128 devices in a mesh: req: 16 (over y, z), mlp: 8 (over x, core).
Axes of the slice: x: 4, y: 4, z: 4, core: 2. Of those that a mesh axis runs over, the one named last changes fastest.
Arguments:
- resid: bfloat16 [2176, 5120], P('req', 'mlp'), may hold values from -180 to 180
- queries: bfloat16 [2176, 5120], P('req', 'mlp'), may hold values from -200 to 200
- new_keys: bfloat16 [2176, 1024], P('req', 'mlp'), may hold values from -6 to 6
- new_values: bfloat16 [2176, 1024], P('req', 'mlp'), may hold values from -6 to 6
- cache_keys: bfloat16 [48, 4096, 1024], P('req', None, 'mlp'), may hold values from -6 to 6
- cache_values: bfloat16 [48, 4096, 1024], P('req', None, 'mlp'), may hold values from -6 to 6
- context_keys: bfloat16 [5, 1024, 1024], P(None, 'req', 'mlp'), may hold values from -6 to 6
- context_values: bfloat16 [5, 1024, 1024], P(None, 'req', 'mlp'), may hold values from -6 to 6
- cache_lengths: int32 [48], P('req'), may hold values from 1 to 4096, 49152 in all
- group_ids: int32 [48], P('req'), may hold values from 0 to 3
- prefix_lengths: int32 [4], replicated, may hold values from 1 to 1024, 2048 in all
- prompt_start: int32 [1], replicated, may hold values from 1 to 1023
- out_weight: bfloat16 [5120, 5120], P('mlp'), may hold values from -1.25 to 1.25
- norm_gain: float32 [5120], P('mlp'), may hold values from 0.5 to 1.5
- gate_weight: bfloat16 [5120, 27648], P(None, ('req', 'mlp')), may hold values from -0.078125 to 0.078125
- up_weight: bfloat16 [5120, 27648], P(None, ('req', 'mlp')), may hold values from -0.078125 to 0.078125
- down_weight: bfloat16 [27648, 5120], P('req', 'mlp'), may hold values from -0.109375 to 0.109375
Outputs:
- out: bfloat16 [2176, 5120], P('req', 'mlp')
The draws below stay inside these ranges and needn't reach their ends.
Inputs may be any that keep to these rules, and one draw needn't show every extreme that they name: `cache_lengths`: one decode request has 4096 valid positions. `prefix_lengths`: one group's prompt has 1024 positions.
All inputs are finite; a program needn't handle non-finite values. No bound on the sum of `cache_lengths` on one device may be relied on, other than what follows from the above.
Results may differ from the reference program's by a relative error of at most 0.019.
Values may be sent and summed in bfloat16 or wider, within the bound.
No kernel may reach another device: no remote copies, remote signals or barrier semaphores. Data moves between devices by JAX's collectives and lax.ppermute only.
A program may use at most 128 MiB of HBM per device.

```python
import math
import jax
import jax.numpy as jnp
import numpy as np
from jax import lax

D = 5120
HQ = 40
KV = 8
HD = 128
FF = 27648
ROWS_DEV = 136
DEC_DEV = 3
GROUPS = 4
CTX = 1024
CACHE = 4096
TOKENS = 2176
DEC = 48
PRE = 2128
NCTX = 5
N_REQ = 16


def paired_keys(key):
    sample = jax.random.normal(jax.random.fold_in(key, 11), (TOKENS, KV * HD), jnp.float32)
    return jnp.clip(sample, -6.0, 6.0)


def draw_new_keys(key, part):
    return paired_keys(key).astype(jnp.bfloat16)


def draw_queries(key, part):
    sample = jnp.clip(jax.random.normal(jax.random.fold_in(key, 17), (TOKENS, HQ * HD), jnp.float32), -6.0, 6.0)
    return sample.astype(jnp.bfloat16)


def draw_cache_keys(key, part):
    sample = jax.random.normal(jax.random.fold_in(key, 19), (DEC, CACHE, KV * HD), jnp.float32)
    return jnp.clip(sample, -6.0, 6.0).astype(jnp.bfloat16)


def draw_resid(key, part):
    sample = jnp.clip(jax.random.normal(jax.random.fold_in(key, 23), (TOKENS, D), jnp.float32), -6.0, 6.0)
    column = jnp.arange(D, dtype=jnp.float32) / D
    row_scale = jnp.exp(jax.random.uniform(jax.random.fold_in(key, 29), (TOKENS, 1), jnp.float32, 0.0, math.log(10.0)))
    column_scale = 0.1 * jnp.exp(math.log(30.0) * column)
    return (sample * column_scale[None, :] * row_scale).astype(jnp.bfloat16)


def set_ends(entries, rng, least, high):
    longest = entries.shape.index(max(entries.shape))
    spots = []
    for shift in (0, 1):
        where = [jax.random.randint(jax.random.fold_in(rng, axis), (), 0, length) for axis, length in enumerate(entries.shape)]
        where[longest] = (where[longest] + shift) % entries.shape[longest]
        spots.append(tuple(where))
    return entries.at[spots[0]].set(least).at[spots[1]].set(high)


def with_spikes(array, rng, source, target, shards_of, factor):
    def block_of(axis_at):
        return (jnp.arange(array.shape[axis_at]) // (array.shape[axis_at] // shards_of)).reshape((-1,) + (1,) * (array.ndim - 1 - axis_at))

    one_side = jax.random.permutation(rng, shards_of)[block_of(target)]
    far = (block_of(target) + shards_of // 2) % shards_of
    return jnp.where((block_of(source) == one_side) | (block_of(source) == far), factor * array, array)


def block_scale(key, extent, split, smallest, high):
    level = 1.0
    for dim, shards_of in split:
        heights = jax.random.uniform(jax.random.fold_in(jax.random.fold_in(key, 6), dim), (shards_of,), jnp.float32, smallest / len(split), high / len(split))
        level = level * jnp.repeat(jnp.exp(heights), extent[dim] // shards_of).reshape((-1,) + (1,) * (len(extent) - 1 - dim))
    return level


def split_up(number_of, total, reach, slope):
    portions = [(1 << 20) // math.isqrt(grade ** slope) + 1 for grade in range(2, number_of + 1)]
    spare, counts = total - reach - (number_of - 1), [1] * (number_of - 1)
    while spare > 0:
        free = [i for i in range(number_of - 1) if counts[i] < reach]
        whole, remaining = sum([portions[i] for i in free]), spare
        for i in free:
            extra = min(reach - counts[i], max(1, remaining * portions[i] // whole), spare)
            counts[i] = counts[i] + extra
            spare = spare - extra
    return np.array([reach] + counts)


def uneven_parts(stream_key, count, total, bound, lean):
    if count == 2:
        one = jax.random.randint(stream_key, (), max(1, total - bound), min(bound, total - 1) + 1)
        return jnp.stack([one, total - one])
    lengths = jnp.asarray(split_up(count, total, bound, lean), jnp.int32)
    pairs = (count - 1) // 2
    source_of, sink = lengths[1:1 + 2 * pairs:2], lengths[2:2 + 2 * pairs:2]
    margin = jnp.minimum(source_of - 1, bound - sink)
    shifted = jax.random.randint(jax.random.fold_in(stream_key, 1), (pairs,), 0, 1 << 20) % (margin + 1)
    lengths = lengths.at[1:1 + 2 * pairs:2].set(source_of - shifted).at[2:2 + 2 * pairs:2].set(sink + shifted)
    return lengths[jax.random.permutation(jax.random.fold_in(stream_key, 2), count)]


def scatter_about(key, shape, width, most, shards=(), kind=jnp.bfloat16):
    entries = width * jax.random.normal(key, shape, jnp.float32)
    if shards:
        entries = entries * block_scale(key, shape, shards, -0.22, 0.18)
    return jnp.clip(entries, -most, most).astype(kind)


def gaussian_with(key, extent, scale, bound, shards, heavy, kind=jnp.bfloat16):
    entries = scale * jax.random.normal(key, extent, jnp.float32)
    if shards:
        entries = entries * block_scale(key, extent, shards, -0.22, 0.18)
    return jnp.clip(with_spikes(entries, jax.random.fold_in(key, 3), *heavy), -bound, bound).astype(kind)


def setup_inputs(seed: int = 0) -> dict:
    streams_of = jax.random.split(jax.random.key(seed), 18)
    return {
        "resid": draw_resid(jax.random.fold_in(streams_of[17], 71), 0),
        "queries": draw_queries(jax.random.fold_in(streams_of[17], 71), 0),
        "new_keys": draw_new_keys(jax.random.fold_in(streams_of[17], 71), 0),
        "new_values": scatter_about(streams_of[3], (TOKENS, KV * HD), 1.0, 6.0, ((0, 16), (1, 8))),
        "cache_keys": draw_cache_keys(jax.random.fold_in(streams_of[17], 71), 0),
        "cache_values": scatter_about(streams_of[5], (DEC, CACHE, KV * HD), 1.0, 6.0, ((0, 16), (2, 8))),
        "context_keys": scatter_about(streams_of[6], (NCTX, CTX, KV * HD), 1.0, 6.0, ((1, 16), (2, 8))),
        "context_values": scatter_about(streams_of[7], (NCTX, CTX, KV * HD), 1.0, 6.0, ((1, 16), (2, 8))),
        "cache_lengths": uneven_parts(streams_of[8], DEC, DEC * CACHE // 4, CACHE, 2).astype(jnp.int32),
        "group_ids": set_ends(jax.random.randint(streams_of[9], (DEC,), 0, GROUPS), jax.random.fold_in(streams_of[9], 1), 0, GROUPS - 1).astype(jnp.int32),
        "prefix_lengths": uneven_parts(streams_of[10], GROUPS, 2 * CTX, CTX, 1).astype(jnp.int32),
        "prompt_start": jax.random.randint(streams_of[11], (1,), 1, CTX).astype(jnp.int32),
        "out_weight": scatter_about(streams_of[12], (HQ * HD, D), (HQ * HD // 256) ** -0.5, 1.25, ((0, 8),)),
        "norm_gain": jnp.clip(1.0 + 0.1 * jax.random.normal(streams_of[13], (D,), jnp.float32), 0.5, 1.5),
        "gate_weight": scatter_about(streams_of[14], (D, FF), D ** -0.5, 0.078125, ((1, 128),)),
        "up_weight": scatter_about(streams_of[15], (D, FF), D ** -0.5, 0.078125, ((1, 128),)),
        "down_weight": gaussian_with(streams_of[16], (FF, D), (FF // 4) ** -0.5, 0.109375, ((0, 16), (1, 8)), (0, 1, 16, 2.0)),
    }


def attend_rows(scores, allowed, values, pattern):
    scores = jnp.where(allowed, scores, -jnp.inf)
    largest = lax.optimization_barrier(jnp.max(scores, axis=-1, keepdims=True))
    exponent = jnp.exp(scores - largest)
    totals = lax.optimization_barrier(jnp.sum(exponent, axis=-1))
    weights = lax.optimization_barrier(exponent.astype(jnp.bfloat16)).astype(jnp.float32)
    summed = jnp.einsum(pattern, weights, values, precision=lax.Precision.HIGHEST)
    return summed / totals[..., None]

def reference(resid, queries, new_keys, new_values, cache_keys, cache_values, context_keys, context_values, cache_lengths, group_ids, prefix_lengths, prompt_start, out_weight, norm_gain, gate_weight, up_weight, down_weight):
    group_size = HQ // KV
    scaling = 1.0 / math.sqrt(HD)
    row_index = jnp.arange(TOKENS, dtype=jnp.int32).reshape(N_REQ, ROWS_DEV)
    decode_rows = row_index[:, :DEC_DEV].reshape(-1)
    prompt_rows = row_index[:, DEC_DEV:].reshape(-1)
    query_all = queries.astype(jnp.float32).reshape(TOKENS, KV, group_size, HD)
    key_all = new_keys.astype(jnp.float32).reshape(TOKENS, KV, HD)
    value_all = new_values.astype(jnp.float32).reshape(TOKENS, KV, HD)
    context_positions = jnp.arange(CTX, dtype=jnp.int32)
    cache_positions = jnp.arange(CACHE, dtype=jnp.int32)

    def decode_one(inputs):
        query_head, own_key, own_value, past_keys, past_values, length, group_index = inputs
        key_list = jnp.concatenate([context_keys[group_index].astype(jnp.float32).reshape(CTX, KV, HD), past_keys.astype(jnp.float32).reshape(CACHE, KV, HD), own_key[None]], 0)
        value_list = jnp.concatenate([context_values[group_index].astype(jnp.float32).reshape(CTX, KV, HD), past_values.astype(jnp.float32).reshape(CACHE, KV, HD), own_value[None]], 0)
        allowed = jnp.concatenate([context_positions < prefix_lengths[group_index], cache_positions < length, jnp.ones((1,), dtype=bool)])
        scores = jnp.einsum('kgd,nkd->kgn', query_head, key_list, precision=lax.Precision.HIGHEST) * scaling
        return attend_rows(scores, allowed[None, None, :], value_list, 'kgn,nkd->kgd')
    decode_out = lax.map(decode_one, (query_all[decode_rows], key_all[decode_rows], value_all[decode_rows], cache_keys, cache_values, cache_lengths, group_ids))
    prompt_keys = jnp.concatenate([context_keys[GROUPS].astype(jnp.float32).reshape(CTX, KV, HD), key_all[prompt_rows]], 0)
    prompt_values = jnp.concatenate([context_values[GROUPS].astype(jnp.float32).reshape(CTX, KV, HD), value_all[prompt_rows]], 0)
    prompt_index = jnp.arange(PRE, dtype=jnp.int32)
    allowed = jnp.concatenate([jnp.broadcast_to((context_positions < prompt_start[0])[None, :], (PRE, CTX)), prompt_index[None, :] <= prompt_index[:, None]], 1)
    prompt_query = query_all[prompt_rows]

    def head_one(head_index):
        query_head = prompt_query[:, head_index]
        key_list = prompt_keys[:, head_index]
        value_list = prompt_values[:, head_index]
        scores = jnp.einsum('jgd,nd->jgn', query_head, key_list, precision=lax.Precision.HIGHEST) * scaling
        return attend_rows(scores, allowed[:, None, :], value_list, 'jgn,nd->jgd')
    prompt_out = jnp.transpose(lax.map(head_one, jnp.arange(KV, dtype=jnp.int32)), (1, 0, 2, 3))
    attended = jnp.zeros((TOKENS, KV, group_size, HD), jnp.float32)
    attended = attended.at[decode_rows].set(decode_out).at[prompt_rows].set(prompt_out)
    attended = attended.reshape(TOKENS, HQ * HD).astype(jnp.bfloat16)
    projected = jnp.dot(attended, out_weight, preferred_element_type=jnp.float32)
    mixed = (resid.astype(jnp.float32) + projected).astype(jnp.bfloat16)
    mixed_wide = mixed.astype(jnp.float32)
    mean_square = lax.optimization_barrier(jnp.mean(mixed_wide * mixed_wide, axis=1, keepdims=True))
    normed = (mixed_wide * lax.rsqrt(mean_square + 1e-06) * norm_gain[None, :]).astype(jnp.bfloat16)
    gate_proj = jnp.dot(normed, gate_weight, preferred_element_type=jnp.float32)
    up_proj = jnp.dot(normed, up_weight, preferred_element_type=jnp.float32)
    hidden = (jax.nn.silu(gate_proj) * up_proj).astype(jnp.bfloat16)
    feed = jnp.dot(hidden, down_weight, preferred_element_type=jnp.float32)
    return (mixed_wide + feed).astype(jnp.bfloat16)
```

```python
import math

import jax
import jax.numpy as jnp
from jax import lax
from jax.sharding import PartitionSpec as P

D = 5120
HQ = 40
KV = 8
HD = 128


NEGATIVE = -1e30


def absorb(carried, scores, allowed, values, pattern):
    running, totals, summed = carried
    scores = jnp.where(allowed, scores, -jnp.inf)
    highest = jnp.maximum(running, jnp.max(scores, axis=-1))
    exponent = jnp.where(allowed, jnp.exp(scores - highest[..., None]), 0.0)
    fading = jnp.exp(running - highest)
    weights = exponent.astype(jnp.bfloat16)
    summed = summed * fading[..., None] + jnp.einsum(
        pattern, weights, values, preferred_element_type=jnp.float32
    )
    totals = totals * fading + jnp.sum(exponent, axis=-1)
    return (highest, totals, summed)


def per_device(
    resid,
    queries,
    new_keys,
    new_values,
    cache_keys,
    cache_values,
    context_keys,
    context_values,
    cache_lengths,
    group_ids,
    prefix_lengths,
    prompt_start,
    out_weight,
    norm_gain,
    gate_weight,
    up_weight,
    down_weight,
):
    rows_here = queries.shape[0]
    decode_count = cache_keys.shape[0]
    prompt_count = rows_here - decode_count
    heads_kv = new_keys.shape[1] // HD
    group_size = HQ // KV
    scaling = 1.0 / math.sqrt(HD)
    cache_span = cache_keys.shape[1]
    context_count = context_keys.shape[0]
    query_rows = queries.reshape(rows_here, heads_kv, group_size, HD)
    query_decode = query_rows[:decode_count]
    query_prompt = query_rows[decode_count:]
    key_rows = new_keys.reshape(rows_here, heads_kv, HD)
    value_rows = new_values.reshape(rows_here, heads_kv, HD)

    def fresh_state(row_count):
        return (
            jnp.full((row_count, heads_kv, group_size), NEGATIVE, jnp.float32),
            jnp.zeros((row_count, heads_kv, group_size), jnp.float32),
            jnp.zeros((row_count, heads_kv, group_size, HD), jnp.float32),
        )

    past_keys = cache_keys.reshape(decode_count, cache_span, heads_kv, HD)
    past_values = cache_values.reshape(decode_count, cache_span, heads_kv, HD)
    scores = (
        jnp.einsum("ikgd,ickd->ikgc", query_decode, past_keys, preferred_element_type=jnp.float32)
        * scaling
    )
    usable = (jnp.arange(cache_span)[None, :] < cache_lengths[:, None])[:, None, None, :]
    decode_state = absorb(fresh_state(decode_count), scores, usable, past_values, "ikgc,ickd->ikgd")
    own_scores = (
        jnp.einsum(
            "ikgd,ikd->ikg",
            query_decode,
            key_rows[:decode_count],
            preferred_element_type=jnp.float32,
        )[..., None]
        * scaling
    )
    decode_state = absorb(
        decode_state,
        own_scores,
        jnp.ones(own_scores.shape, dtype=bool),
        value_rows[:decode_count][:, None],
        "ikgc,ickd->ikgd",
    )
    prompt_length = prompt_start[0]
    prefix_here = prefix_lengths[group_ids]
    state_decode = decode_state
    state_prompt = fresh_state(prompt_count)
    req_count = lax.axis_size("req")
    context_rows = context_keys.shape[1]
    packed = jnp.concatenate(
        [
            context_keys.reshape(context_count * context_rows, heads_kv * HD),
            context_values.reshape(context_count * context_rows, heads_kv * HD),
            new_keys,
            new_values,
        ],
        0,
    )
    gathered = lax.all_gather(packed, "req", axis=0, tiled=False)
    context_span = context_count * context_rows

    def context_of(offset):
        piece = gathered[:, offset : offset + context_span]
        piece = piece.reshape(req_count, context_count, context_rows, heads_kv * HD)
        return jnp.transpose(piece, (1, 0, 2, 3)).reshape(
            context_count, req_count * context_rows, heads_kv * HD
        )

    def prompt_of(offset):
        piece = gathered[:, offset : offset + rows_here][:, decode_count:]
        return piece.reshape(req_count * prompt_count, heads_kv * HD)

    key_block = context_of(0)
    value_block = context_of(context_span)
    extent = key_block.shape[1]
    positions = jnp.arange(extent)
    key_split = key_block.reshape(context_count, extent, heads_kv, HD)
    value_split = value_block.reshape(context_count, extent, heads_kv, HD)
    chosen_keys = key_split[group_ids]
    chosen_values = value_split[group_ids]
    block_scores = (
        jnp.einsum("ikgd,ickd->ikgc", query_decode, chosen_keys, preferred_element_type=jnp.float32)
        * scaling
    )
    block_usable = (positions[None, :] < prefix_here[:, None])[:, None, None, :]
    state_decode = absorb(
        state_decode, block_scores, block_usable, chosen_values, "ikgc,ickd->ikgd"
    )
    block_scores = (
        jnp.einsum(
            "jkgd,ckd->jkgc",
            query_prompt,
            key_split[context_count - 1],
            preferred_element_type=jnp.float32,
        )
        * scaling
    )
    block_usable = (positions < prompt_length)[None, None, None, :]
    state_prompt = absorb(
        state_prompt, block_scores, block_usable, value_split[context_count - 1], "jkgc,ckd->jkgd"
    )
    prompt_state = state_prompt
    own_positions = lax.axis_index("req") * prompt_count + jnp.arange(prompt_count, dtype=jnp.int32)
    key_block = prompt_of(2 * context_span)
    value_block = prompt_of(2 * context_span + rows_here)
    extent = key_block.shape[0]
    positions = jnp.arange(extent, dtype=jnp.int32)
    block_scores = (
        jnp.einsum(
            "jkgd,ckd->jkgc",
            query_prompt,
            key_block.reshape(extent, heads_kv, HD),
            preferred_element_type=jnp.float32,
        )
        * scaling
    )
    block_usable = (positions[None, :] <= own_positions[:, None])[:, None, None, :]
    prompt_state = absorb(
        prompt_state,
        block_scores,
        block_usable,
        value_block.reshape(extent, heads_kv, HD),
        "jkgc,ckd->jkgd",
    )

    def finish(carried):
        return (carried[2] / carried[1][..., None]).astype(jnp.bfloat16)

    attended = jnp.concatenate([finish(state_decode), finish(prompt_state)], 0).reshape(
        rows_here, heads_kv * group_size * HD
    )
    mlp_count = lax.axis_size("mlp")
    head_partial = jnp.dot(attended, out_weight, preferred_element_type=jnp.float32)
    pieces = lax.all_to_all(
        head_partial.astype(jnp.bfloat16), "mlp", 1, 0, tiled=True
    )
    projected = jnp.sum(
        pieces.reshape(mlp_count, rows_here, -1).astype(jnp.float32), axis=0
    )
    mixed = (resid.astype(jnp.float32) + projected).astype(jnp.bfloat16)
    mixed_wide = mixed.astype(jnp.float32)
    mixed_rows = lax.all_gather(mixed, "mlp", axis=1, tiled=True).astype(jnp.float32)
    square_total = jnp.sum(mixed_rows * mixed_rows, axis=1)
    half = D // 2
    side = lax.axis_index("mlp") % 2
    own_half = lax.dynamic_slice_in_dim(mixed_rows, side * half, half, axis=1)
    own_gain = lax.dynamic_slice_in_dim(norm_gain, side * half, half, axis=0)
    normed = (
        own_half * lax.rsqrt(square_total / D + 1e-06)[:, None] * own_gain[None, :]
    ).astype(jnp.bfloat16)
    near_rows = lax.all_gather(normed, "req", axis=0, tiled=True)
    pairs = [(i, i ^ 1) for i in range(mlp_count)]
    far_rows = lax.ppermute(near_rows, "mlp", pairs)

    def project(weight):
        near_weight = lax.dynamic_slice_in_dim(weight, side * half, half, axis=0)
        far_weight = lax.dynamic_slice_in_dim(weight, (1 - side) * half, half, axis=0)
        return jnp.dot(near_rows, near_weight, preferred_element_type=jnp.float32) + jnp.dot(
            far_rows, far_weight, preferred_element_type=jnp.float32
        )

    gate_proj = project(gate_weight)
    up_proj = project(up_weight)
    hidden = (jax.nn.silu(gate_proj) * up_proj).astype(jnp.bfloat16)
    hidden_block = lax.all_gather(hidden, "mlp", axis=1, tiled=True)
    down_partial = jnp.dot(hidden_block, down_weight, preferred_element_type=jnp.float32)
    req_pieces = lax.all_to_all(down_partial.astype(jnp.bfloat16), "req", 0, 0, tiled=True)
    feed = jnp.sum(
        req_pieces.reshape(req_count, rows_here, -1).astype(jnp.float32), axis=0
    )
    return (mixed_wide + feed).astype(jnp.bfloat16)


def solution(mesh):
    return jax.shard_map(
        per_device,
        mesh=mesh,
        in_specs=(
            P("req", "mlp"),
            P("req", "mlp"),
            P("req", "mlp"),
            P("req", "mlp"),
            P("req", None, "mlp"),
            P("req", None, "mlp"),
            P(None, "req", "mlp"),
            P(None, "req", "mlp"),
            P("req"),
            P("req"),
            P(),
            P(),
            P("mlp", None),
            P(),
            P(None, ("req", "mlp")),
            P(None, ("req", "mlp")),
            P("req", "mlp"),
        ),
        out_specs=P("req", "mlp"),
        check_vma=False,
    )
```

```python
import math

import jax
import jax.numpy as jnp
from jax import lax
from jax.sharding import PartitionSpec as P

D = 5120
HQ = 40
KV = 8
HD = 128


NEGATIVE = -1e30


def absorb(carried, scores, allowed, values, pattern):
    running, totals, summed = carried
    scores = jnp.where(allowed, scores, -jnp.inf)
    highest = jnp.maximum(running, jnp.max(scores, axis=-1))
    exponent = jnp.where(allowed, jnp.exp(scores - highest[..., None]), 0.0)
    fading = jnp.exp(running - highest)
    weights = exponent.astype(jnp.bfloat16)
    summed = summed * fading[..., None] + jnp.einsum(
        pattern, weights, values, preferred_element_type=jnp.float32
    )
    totals = totals * fading + jnp.sum(exponent, axis=-1)
    return (highest, totals, summed)


def per_device(
    resid,
    queries,
    new_keys,
    new_values,
    cache_keys,
    cache_values,
    context_keys,
    context_values,
    cache_lengths,
    group_ids,
    prefix_lengths,
    prompt_start,
    out_weight,
    norm_gain,
    gate_weight,
    up_weight,
    down_weight,
):
    rows_here = queries.shape[0]
    decode_count = cache_keys.shape[0]
    prompt_count = rows_here - decode_count
    heads_kv = new_keys.shape[1] // HD
    group_size = HQ // KV
    scaling = 1.0 / math.sqrt(HD)
    cache_span = cache_keys.shape[1]
    context_count = context_keys.shape[0]
    query_rows = queries.reshape(rows_here, heads_kv, group_size, HD)
    query_decode = query_rows[:decode_count]
    query_prompt = query_rows[decode_count:]
    key_rows = new_keys.reshape(rows_here, heads_kv, HD)
    value_rows = new_values.reshape(rows_here, heads_kv, HD)

    def fresh_state(row_count):
        return (
            jnp.full((row_count, heads_kv, group_size), NEGATIVE, jnp.float32),
            jnp.zeros((row_count, heads_kv, group_size), jnp.float32),
            jnp.zeros((row_count, heads_kv, group_size, HD), jnp.float32),
        )

    past_keys = cache_keys.reshape(decode_count, cache_span, heads_kv, HD)
    past_values = cache_values.reshape(decode_count, cache_span, heads_kv, HD)
    scores = (
        jnp.einsum("ikgd,ickd->ikgc", query_decode, past_keys, preferred_element_type=jnp.float32)
        * scaling
    )
    usable = (jnp.arange(cache_span)[None, :] < cache_lengths[:, None])[:, None, None, :]
    decode_state = absorb(fresh_state(decode_count), scores, usable, past_values, "ikgc,ickd->ikgd")
    own_scores = (
        jnp.einsum(
            "ikgd,ikd->ikg",
            query_decode,
            key_rows[:decode_count],
            preferred_element_type=jnp.float32,
        )[..., None]
        * scaling
    )
    decode_state = absorb(
        decode_state,
        own_scores,
        jnp.ones(own_scores.shape, dtype=bool),
        value_rows[:decode_count][:, None],
        "ikgc,ickd->ikgd",
    )
    prompt_length = prompt_start[0]
    prefix_here = prefix_lengths[group_ids]
    state_decode = decode_state
    state_prompt = fresh_state(prompt_count)
    req_count = lax.axis_size("req")
    context_rows = context_keys.shape[1]
    packed = jnp.concatenate(
        [
            context_keys.reshape(context_count * context_rows, heads_kv * HD),
            context_values.reshape(context_count * context_rows, heads_kv * HD),
            new_keys,
            new_values,
        ],
        0,
    )
    gathered = lax.all_gather(packed, "req", axis=0, tiled=False)
    context_span = context_count * context_rows

    def context_of(offset):
        piece = gathered[:, offset : offset + context_span]
        piece = piece.reshape(req_count, context_count, context_rows, heads_kv * HD)
        return jnp.transpose(piece, (1, 0, 2, 3)).reshape(
            context_count, req_count * context_rows, heads_kv * HD
        )

    def prompt_of(offset):
        piece = gathered[:, offset : offset + rows_here][:, decode_count:]
        return piece.reshape(req_count * prompt_count, heads_kv * HD)

    key_block = context_of(0)
    value_block = context_of(context_span)
    extent = key_block.shape[1]
    positions = jnp.arange(extent)
    key_split = key_block.reshape(context_count, extent, heads_kv, HD)
    value_split = value_block.reshape(context_count, extent, heads_kv, HD)
    chosen_keys = key_split[group_ids]
    chosen_values = value_split[group_ids]
    block_scores = (
        jnp.einsum("ikgd,ickd->ikgc", query_decode, chosen_keys, preferred_element_type=jnp.float32)
        * scaling
    )
    block_usable = (positions[None, :] < prefix_here[:, None])[:, None, None, :]
    state_decode = absorb(
        state_decode, block_scores, block_usable, chosen_values, "ikgc,ickd->ikgd"
    )
    block_scores = (
        jnp.einsum(
            "jkgd,ckd->jkgc",
            query_prompt,
            key_split[context_count - 1],
            preferred_element_type=jnp.float32,
        )
        * scaling
    )
    block_usable = (positions < prompt_length)[None, None, None, :]
    state_prompt = absorb(
        state_prompt, block_scores, block_usable, value_split[context_count - 1], "jkgc,ckd->jkgd"
    )
    prompt_state = state_prompt
    own_positions = lax.axis_index("req") * prompt_count + jnp.arange(prompt_count, dtype=jnp.int32)
    key_block = prompt_of(2 * context_span)
    value_block = prompt_of(2 * context_span + rows_here)
    extent = key_block.shape[0]
    positions = jnp.arange(extent, dtype=jnp.int32)
    block_scores = (
        jnp.einsum(
            "jkgd,ckd->jkgc",
            query_prompt,
            key_block.reshape(extent, heads_kv, HD),
            preferred_element_type=jnp.float32,
        )
        * scaling
    )
    block_usable = (positions[None, :] <= own_positions[:, None])[:, None, None, :]
    prompt_state = absorb(
        prompt_state,
        block_scores,
        block_usable,
        value_block.reshape(extent, heads_kv, HD),
        "jkgc,ckd->jkgd",
    )

    def finish(carried):
        return (carried[2] / carried[1][..., None]).astype(jnp.bfloat16)

    attended = jnp.concatenate([finish(state_decode), finish(prompt_state)], 0).reshape(
        rows_here, heads_kv * group_size * HD
    )
    mlp_count = lax.axis_size("mlp")
    head_partial = jnp.dot(attended, out_weight, preferred_element_type=jnp.float32)
    pieces = lax.all_to_all(
        head_partial.astype(jnp.bfloat16), "mlp", 1, 0, tiled=True
    )
    projected = jnp.sum(
        pieces.reshape(mlp_count, rows_here, -1).astype(jnp.float32), axis=0
    )
    mixed = (resid.astype(jnp.float32) + projected).astype(jnp.bfloat16)
    mixed_wide = mixed.astype(jnp.float32)
    gain_pieces = []
    remainder = norm_gain
    for _ in range(3):
        piece = remainder.astype(jnp.bfloat16)
        gain_pieces.append(piece)
        remainder = remainder - piece.astype(jnp.float32)
    with_gain = jnp.concatenate([mixed, jnp.stack(gain_pieces, 0)], 0)
    gathered_rows = lax.all_gather(with_gain, "mlp", axis=1, tiled=True).astype(jnp.float32)
    mixed_rows = gathered_rows[:rows_here]
    full_gain = (gathered_rows[rows_here] + gathered_rows[rows_here + 1]) + gathered_rows[rows_here + 2]
    square_total = jnp.sum(mixed_rows * mixed_rows, axis=1)
    half = D // 2
    side = lax.axis_index("mlp") % 2
    own_half = lax.dynamic_slice_in_dim(mixed_rows, side * half, half, axis=1)
    own_gain = lax.dynamic_slice_in_dim(full_gain, side * half, half, axis=0)
    normed = (
        own_half * lax.rsqrt(square_total / D + 1e-06)[:, None] * own_gain[None, :]
    ).astype(jnp.bfloat16)
    pairs = [(i, i ^ 1) for i in range(mlp_count)]

    def halves(weight):
        return (
            lax.dynamic_slice_in_dim(weight, side * half, half, axis=0),
            lax.dynamic_slice_in_dim(weight, (1 - side) * half, half, axis=0),
        )

    gate_near, gate_far = halves(gate_weight)
    up_near, up_far = halves(up_weight)
    chunk_count = 2
    chunk_rows = rows_here // chunk_count
    feeds = []
    for chunk in range(chunk_count):
        rows = normed[chunk * chunk_rows : (chunk + 1) * chunk_rows]
        near_rows = lax.all_gather(rows, "req", axis=0, tiled=True)
        far_rows = lax.ppermute(near_rows, "mlp", pairs)
        gate_proj = jnp.dot(near_rows, gate_near, preferred_element_type=jnp.float32) + jnp.dot(
            far_rows, gate_far, preferred_element_type=jnp.float32
        )
        up_proj = jnp.dot(near_rows, up_near, preferred_element_type=jnp.float32) + jnp.dot(
            far_rows, up_far, preferred_element_type=jnp.float32
        )
        hidden = (jax.nn.silu(gate_proj) * up_proj).astype(jnp.bfloat16)
        hidden_block = lax.all_gather(hidden, "mlp", axis=1, tiled=True)
        down_partial = jnp.dot(hidden_block, down_weight, preferred_element_type=jnp.float32)
        req_pieces = lax.all_to_all(down_partial.astype(jnp.bfloat16), "req", 0, 0, tiled=True)
        feeds.append(
            jnp.sum(req_pieces.reshape(req_count, chunk_rows, -1).astype(jnp.float32), axis=0)
        )
    feed = jnp.concatenate(feeds, 0)
    return (mixed_wide + feed).astype(jnp.bfloat16)


def solution(mesh):
    return jax.shard_map(
        per_device,
        mesh=mesh,
        in_specs=(
            P("req", "mlp"),
            P("req", "mlp"),
            P("req", "mlp"),
            P("req", "mlp"),
            P("req", None, "mlp"),
            P("req", None, "mlp"),
            P(None, "req", "mlp"),
            P(None, "req", "mlp"),
            P("req"),
            P("req"),
            P(),
            P(),
            P("mlp", None),
            P("mlp"),
            P(None, ("req", "mlp")),
            P(None, ("req", "mlp")),
            P("req", "mlp"),
        ),
        out_specs=P("req", "mlp"),
        check_vma=False,
    )
```

```python
import math

import jax
import jax.numpy as jnp
from jax import lax
from jax.sharding import PartitionSpec as P

D = 5120
HQ = 40
KV = 8
HD = 128


NEGATIVE = -1e30


def absorb(carried, scores, allowed, values, pattern):
    running, totals, summed = carried
    scores = jnp.where(allowed, scores, -jnp.inf)
    highest = jnp.maximum(running, jnp.max(scores, axis=-1))
    exponent = jnp.where(allowed, jnp.exp(scores - highest[..., None]), 0.0)
    fading = jnp.exp(running - highest)
    weights = exponent.astype(jnp.bfloat16)
    summed = summed * fading[..., None] + jnp.einsum(
        pattern, weights, values, preferred_element_type=jnp.float32
    )
    totals = totals * fading + jnp.sum(exponent, axis=-1)
    return (highest, totals, summed)


def per_device(
    resid,
    queries,
    new_keys,
    new_values,
    cache_keys,
    cache_values,
    context_keys,
    context_values,
    cache_lengths,
    group_ids,
    prefix_lengths,
    prompt_start,
    out_weight,
    norm_gain,
    gate_weight,
    up_weight,
    down_weight,
):
    rows_here = queries.shape[0]
    decode_count = cache_keys.shape[0]
    prompt_count = rows_here - decode_count
    heads_kv = new_keys.shape[1] // HD
    group_size = HQ // KV
    scaling = 1.0 / math.sqrt(HD)
    cache_span = cache_keys.shape[1]
    context_count = context_keys.shape[0]
    query_rows = queries.reshape(rows_here, heads_kv, group_size, HD)
    query_decode = query_rows[:decode_count]
    query_prompt = query_rows[decode_count:]
    key_rows = new_keys.reshape(rows_here, heads_kv, HD)
    value_rows = new_values.reshape(rows_here, heads_kv, HD)

    def fresh_state(row_count):
        return (
            jnp.full((row_count, heads_kv, group_size), NEGATIVE, jnp.float32),
            jnp.zeros((row_count, heads_kv, group_size), jnp.float32),
            jnp.zeros((row_count, heads_kv, group_size, HD), jnp.float32),
        )

    past_keys = cache_keys.reshape(decode_count, cache_span, heads_kv, HD)
    past_values = cache_values.reshape(decode_count, cache_span, heads_kv, HD)
    scores = (
        jnp.einsum("ikgd,ickd->ikgc", query_decode, past_keys, preferred_element_type=jnp.float32)
        * scaling
    )
    usable = (jnp.arange(cache_span)[None, :] < cache_lengths[:, None])[:, None, None, :]
    decode_state = absorb(fresh_state(decode_count), scores, usable, past_values, "ikgc,ickd->ikgd")
    own_scores = (
        jnp.einsum(
            "ikgd,ikd->ikg",
            query_decode,
            key_rows[:decode_count],
            preferred_element_type=jnp.float32,
        )[..., None]
        * scaling
    )
    decode_state = absorb(
        decode_state,
        own_scores,
        jnp.ones(own_scores.shape, dtype=bool),
        value_rows[:decode_count][:, None],
        "ikgc,ickd->ikgd",
    )
    prompt_length = prompt_start[0]
    prefix_here = prefix_lengths[group_ids]
    state_decode = decode_state
    state_prompt = fresh_state(prompt_count)
    req_count = lax.axis_size("req")
    context_rows = context_keys.shape[1]
    packed = jnp.concatenate(
        [
            context_keys.reshape(context_count * context_rows, heads_kv * HD),
            context_values.reshape(context_count * context_rows, heads_kv * HD),
            new_keys,
            new_values,
        ],
        0,
    )
    gathered = lax.all_gather(packed, "req", axis=0, tiled=False)
    context_span = context_count * context_rows

    def context_of(offset):
        piece = gathered[:, offset : offset + context_span]
        piece = piece.reshape(req_count, context_count, context_rows, heads_kv * HD)
        return jnp.transpose(piece, (1, 0, 2, 3)).reshape(
            context_count, req_count * context_rows, heads_kv * HD
        )

    def prompt_of(offset):
        piece = gathered[:, offset : offset + rows_here][:, decode_count:]
        return piece.reshape(req_count * prompt_count, heads_kv * HD)

    key_block = context_of(0)
    value_block = context_of(context_span)
    extent = key_block.shape[1]
    positions = jnp.arange(extent)
    key_split = key_block.reshape(context_count, extent, heads_kv, HD)
    value_split = value_block.reshape(context_count, extent, heads_kv, HD)
    chosen_keys = key_split[group_ids]
    chosen_values = value_split[group_ids]
    block_scores = (
        jnp.einsum("ikgd,ickd->ikgc", query_decode, chosen_keys, preferred_element_type=jnp.float32)
        * scaling
    )
    block_usable = (positions[None, :] < prefix_here[:, None])[:, None, None, :]
    state_decode = absorb(
        state_decode, block_scores, block_usable, chosen_values, "ikgc,ickd->ikgd"
    )
    block_scores = (
        jnp.einsum(
            "jkgd,ckd->jkgc",
            query_prompt,
            key_split[context_count - 1],
            preferred_element_type=jnp.float32,
        )
        * scaling
    )
    block_usable = (positions < prompt_length)[None, None, None, :]
    state_prompt = absorb(
        state_prompt, block_scores, block_usable, value_split[context_count - 1], "jkgc,ckd->jkgd"
    )
    prompt_state = state_prompt
    own_positions = lax.axis_index("req") * prompt_count + jnp.arange(prompt_count, dtype=jnp.int32)
    key_block = prompt_of(2 * context_span)
    value_block = prompt_of(2 * context_span + rows_here)
    extent = key_block.shape[0]
    positions = jnp.arange(extent, dtype=jnp.int32)
    block_scores = (
        jnp.einsum(
            "jkgd,ckd->jkgc",
            query_prompt,
            key_block.reshape(extent, heads_kv, HD),
            preferred_element_type=jnp.float32,
        )
        * scaling
    )
    block_usable = (positions[None, :] <= own_positions[:, None])[:, None, None, :]
    prompt_state = absorb(
        prompt_state,
        block_scores,
        block_usable,
        value_block.reshape(extent, heads_kv, HD),
        "jkgc,ckd->jkgd",
    )

    def finish(carried):
        return (carried[2] / carried[1][..., None]).astype(jnp.bfloat16)

    attended = jnp.concatenate([finish(state_decode), finish(prompt_state)], 0).reshape(
        rows_here, heads_kv * group_size * HD
    )
    mlp_count = lax.axis_size("mlp")
    head_partial = jnp.dot(attended, out_weight, preferred_element_type=jnp.float32)
    pieces = lax.all_to_all(
        head_partial.astype(jnp.bfloat16), "mlp", 1, 0, tiled=True
    )
    projected = jnp.sum(
        pieces.reshape(mlp_count, rows_here, -1).astype(jnp.float32), axis=0
    )
    mixed = (resid.astype(jnp.float32) + projected).astype(jnp.bfloat16)
    mixed_wide = mixed.astype(jnp.float32)
    gain_pieces = []
    remainder = norm_gain
    for _ in range(3):
        piece = remainder.astype(jnp.bfloat16)
        gain_pieces.append(piece)
        remainder = remainder - piece.astype(jnp.float32)
    with_gain = jnp.concatenate([mixed, jnp.stack(gain_pieces, 0)], 0)
    gathered_rows = lax.all_gather(with_gain, "mlp", axis=1, tiled=True).astype(jnp.float32)
    mixed_rows = gathered_rows[:rows_here]
    full_gain = (gathered_rows[rows_here] + gathered_rows[rows_here + 1]) + gathered_rows[rows_here + 2]
    square_total = jnp.sum(mixed_rows * mixed_rows, axis=1)
    half = D // 2
    side = lax.axis_index("mlp") % 2
    own_half = lax.dynamic_slice_in_dim(mixed_rows, side * half, half, axis=1)
    own_gain = lax.dynamic_slice_in_dim(full_gain, side * half, half, axis=0)
    normed = (
        own_half * lax.rsqrt(square_total / D + 1e-06)[:, None] * own_gain[None, :]
    ).astype(jnp.bfloat16)
    pairs = [(i, i ^ 1) for i in range(mlp_count)]

    def halves(weight):
        return (
            lax.dynamic_slice_in_dim(weight, side * half, half, axis=0),
            lax.dynamic_slice_in_dim(weight, (1 - side) * half, half, axis=0),
        )

    req_split = (half * 7 // 10) // 128 * 128

    def gathered(block):
        spread = block.shape[1] - req_split
        copies = jnp.broadcast_to(block[:, req_split:][None], (req_count, rows_here, spread))
        return (
            lax.all_gather(block[:, :req_split], "req", axis=0, tiled=True),
            lax.all_to_all(
                copies.reshape(req_count * rows_here, spread), "req", 0, 0, tiled=True
            ),
        )

    near_rows = gathered(normed)
    far_rows = tuple(lax.ppermute(part, "mlp", pairs) for part in near_rows)

    def project(weight):
        near_weight, far_weight = halves(weight)
        total = None
        for rows, part_weight in ((near_rows, near_weight), (far_rows, far_weight)):
            for index, lower, upper in ((0, 0, req_split), (1, req_split, half)):
                term = jnp.dot(
                    rows[index], part_weight[lower:upper], preferred_element_type=jnp.float32
                )
                total = term if total is None else total + term
        return total

    gate_proj = project(gate_weight)
    up_proj = project(up_weight)
    hidden = (jax.nn.silu(gate_proj) * up_proj).astype(jnp.bfloat16)
    hidden_block = lax.all_gather(hidden, "mlp", axis=1, tiled=True)
    down_partial = jnp.dot(hidden_block, down_weight, preferred_element_type=jnp.float32)
    req_pieces = lax.all_to_all(down_partial.astype(jnp.bfloat16), "req", 0, 0, tiled=True)
    feed = jnp.sum(
        req_pieces.reshape(req_count, rows_here, -1).astype(jnp.float32), axis=0
    )
    return (mixed_wide + feed).astype(jnp.bfloat16)


def solution(mesh):
    return jax.shard_map(
        per_device,
        mesh=mesh,
        in_specs=(
            P("req", "mlp"),
            P("req", "mlp"),
            P("req", "mlp"),
            P("req", "mlp"),
            P("req", None, "mlp"),
            P("req", None, "mlp"),
            P(None, "req", "mlp"),
            P(None, "req", "mlp"),
            P("req"),
            P("req"),
            P(),
            P(),
            P("mlp", None),
            P("mlp"),
            P(None, ("req", "mlp")),
            P(None, ("req", "mlp")),
            P("req", "mlp"),
        ),
        out_specs=P("req", "mlp"),
        check_vma=False,
    )
```

```python
import math

import jax
import jax.numpy as jnp
from jax import lax
from jax.sharding import PartitionSpec as P


D = 5120
HQ = 40
KV = 8
HD = 128


NEGATIVE = -1e30


def absorb(carried, scores, allowed, values, pattern):
    running, totals, summed = carried
    scores = jnp.where(allowed, scores, -jnp.inf)
    highest = jnp.maximum(running, jnp.max(scores, axis=-1))
    exponent = jnp.where(allowed, jnp.exp(scores - highest[..., None]), 0.0)
    fading = jnp.exp(running - highest)
    weights = exponent.astype(jnp.bfloat16)
    summed = summed * fading[..., None] + jnp.einsum(
        pattern, weights, values, preferred_element_type=jnp.float32
    )
    totals = totals * fading + jnp.sum(exponent, axis=-1)
    return (highest, totals, summed)


def per_device(
    resid,
    queries,
    new_keys,
    new_values,
    cache_keys,
    cache_values,
    context_keys,
    context_values,
    cache_lengths,
    group_ids,
    prefix_lengths,
    prompt_start,
    out_weight,
    norm_gain,
    gate_weight,
    up_weight,
    down_weight,
):
    rows_here = queries.shape[0]
    decode_count = cache_keys.shape[0]
    prompt_count = rows_here - decode_count
    heads_kv = new_keys.shape[1] // HD
    group_size = HQ // KV
    scaling = 1.0 / math.sqrt(HD)
    cache_span = cache_keys.shape[1]
    context_count = context_keys.shape[0]
    query_rows = queries.reshape(rows_here, heads_kv, group_size, HD)
    query_decode = query_rows[:decode_count]
    query_prompt = query_rows[decode_count:]
    key_rows = new_keys.reshape(rows_here, heads_kv, HD)
    value_rows = new_values.reshape(rows_here, heads_kv, HD)

    def fresh_state(row_count):
        return (
            jnp.full((row_count, heads_kv, group_size), NEGATIVE, jnp.float32),
            jnp.zeros((row_count, heads_kv, group_size), jnp.float32),
            jnp.zeros((row_count, heads_kv, group_size, HD), jnp.float32),
        )

    swap_with = [(i, i ^ 2) for i in range(lax.axis_size("mlp"))]
    gate_other = lax.ppermute(gate_weight, "mlp", swap_with)
    up_other = lax.ppermute(up_weight, "mlp", swap_with)
    past_keys = cache_keys.reshape(decode_count, cache_span, heads_kv, HD)
    past_values = cache_values.reshape(decode_count, cache_span, heads_kv, HD)
    scores = (
        jnp.einsum("ikgd,ickd->ikgc", query_decode, past_keys, preferred_element_type=jnp.float32)
        * scaling
    )
    usable = (jnp.arange(cache_span)[None, :] < cache_lengths[:, None])[:, None, None, :]
    decode_state = absorb(fresh_state(decode_count), scores, usable, past_values, "ikgc,ickd->ikgd")
    own_scores = (
        jnp.einsum(
            "ikgd,ikd->ikg",
            query_decode,
            key_rows[:decode_count],
            preferred_element_type=jnp.float32,
        )[..., None]
        * scaling
    )
    decode_state = absorb(
        decode_state,
        own_scores,
        jnp.ones(own_scores.shape, dtype=bool),
        value_rows[:decode_count][:, None],
        "ikgc,ickd->ikgd",
    )
    prompt_length = prompt_start[0]
    prefix_here = prefix_lengths[group_ids]
    state_decode = decode_state
    state_prompt = fresh_state(prompt_count)
    req_count = lax.axis_size("req")
    context_rows = context_keys.shape[1]
    packed = jnp.concatenate(
        [
            context_keys.reshape(context_count * context_rows, heads_kv * HD),
            context_values.reshape(context_count * context_rows, heads_kv * HD),
            new_keys,
            new_values,
        ],
        0,
    )
    gathered = lax.all_gather(packed, "req", axis=0, tiled=False)
    context_span = context_count * context_rows

    def context_of(offset):
        piece = gathered[:, offset : offset + context_span]
        piece = piece.reshape(req_count, context_count, context_rows, heads_kv * HD)
        return jnp.transpose(piece, (1, 0, 2, 3)).reshape(
            context_count, req_count * context_rows, heads_kv * HD
        )

    def prompt_of(offset):
        piece = gathered[:, offset : offset + rows_here][:, decode_count:]
        return piece.reshape(req_count * prompt_count, heads_kv * HD)

    key_block = context_of(0)
    value_block = context_of(context_span)
    extent = key_block.shape[1]
    positions = jnp.arange(extent)
    key_split = key_block.reshape(context_count, extent, heads_kv, HD)
    value_split = value_block.reshape(context_count, extent, heads_kv, HD)
    chosen_keys = key_split[group_ids]
    chosen_values = value_split[group_ids]
    block_scores = (
        jnp.einsum("ikgd,ickd->ikgc", query_decode, chosen_keys, preferred_element_type=jnp.float32)
        * scaling
    )
    block_usable = (positions[None, :] < prefix_here[:, None])[:, None, None, :]
    state_decode = absorb(
        state_decode, block_scores, block_usable, chosen_values, "ikgc,ickd->ikgd"
    )
    block_scores = (
        jnp.einsum(
            "jkgd,ckd->jkgc",
            query_prompt,
            key_split[context_count - 1],
            preferred_element_type=jnp.float32,
        )
        * scaling
    )
    block_usable = (positions < prompt_length)[None, None, None, :]
    state_prompt = absorb(
        state_prompt, block_scores, block_usable, value_split[context_count - 1], "jkgc,ckd->jkgd"
    )
    prompt_state = state_prompt
    own_positions = lax.axis_index("req") * prompt_count + jnp.arange(prompt_count, dtype=jnp.int32)
    key_block = prompt_of(2 * context_span)
    value_block = prompt_of(2 * context_span + rows_here)
    extent = key_block.shape[0]
    positions = jnp.arange(extent, dtype=jnp.int32)
    block_scores = (
        jnp.einsum(
            "jkgd,ckd->jkgc",
            query_prompt,
            key_block.reshape(extent, heads_kv, HD),
            preferred_element_type=jnp.float32,
        )
        * scaling
    )
    block_usable = (positions[None, :] <= own_positions[:, None])[:, None, None, :]
    prompt_state = absorb(
        prompt_state,
        block_scores,
        block_usable,
        value_block.reshape(extent, heads_kv, HD),
        "jkgc,ckd->jkgd",
    )

    def finish(carried):
        return (carried[2] / carried[1][..., None]).astype(jnp.bfloat16)

    attended = jnp.concatenate([finish(state_decode), finish(prompt_state)], 0).reshape(
        rows_here, heads_kv * group_size * HD
    )
    mlp_count = lax.axis_size("mlp")
    head_partial = jnp.dot(attended, out_weight, preferred_element_type=jnp.float32)
    pieces = lax.all_to_all(
        head_partial.astype(jnp.bfloat16), "mlp", 1, 0, tiled=True
    )
    projected = jnp.sum(
        pieces.reshape(mlp_count, rows_here, -1).astype(jnp.float32), axis=0
    )
    mixed = (resid.astype(jnp.float32) + projected).astype(jnp.bfloat16)
    mixed_wide = mixed.astype(jnp.float32)
    gain_pieces = []
    remainder = norm_gain
    for _ in range(3):
        piece = remainder.astype(jnp.bfloat16)
        gain_pieces.append(piece)
        remainder = remainder - piece.astype(jnp.float32)
    with_gain = jnp.concatenate([mixed, jnp.stack(gain_pieces, 0)], 0)
    gathered_rows = lax.all_gather(with_gain, "mlp", axis=1, tiled=True).astype(jnp.float32)
    mixed_rows = gathered_rows[:rows_here]
    full_gain = (gathered_rows[rows_here] + gathered_rows[rows_here + 1]) + gathered_rows[rows_here + 2]
    square_total = jnp.sum(mixed_rows * mixed_rows, axis=1)
    half = D // 2
    side = lax.axis_index("mlp") % 2
    own_half = lax.dynamic_slice_in_dim(mixed_rows, side * half, half, axis=1)
    own_gain = lax.dynamic_slice_in_dim(full_gain, side * half, half, axis=0)
    normed = (
        own_half * lax.rsqrt(square_total / D + 1e-06)[:, None] * own_gain[None, :]
    ).astype(jnp.bfloat16)
    pairs = [(i, i ^ 1) for i in range(mlp_count)]
    parity = (lax.axis_index("mlp") // 2) % 2
    gate_pair = jnp.concatenate([gate_weight, gate_other], 1)
    up_pair = jnp.concatenate([up_weight, up_other], 1)

    def halves(weight):
        return (
            lax.dynamic_slice_in_dim(weight, side * half, half, axis=0),
            lax.dynamic_slice_in_dim(weight, (1 - side) * half, half, axis=0),
        )

    row_half = rows_here // 2
    my_rows = lax.dynamic_slice_in_dim(normed, parity * row_half, row_half, axis=0)
    near_rows = lax.all_gather(my_rows, "req", axis=0, tiled=True)
    far_rows = lax.ppermute(near_rows, "mlp", pairs)

    def project(weight):
        near_weight, far_weight = halves(weight)
        return jnp.dot(near_rows, near_weight, preferred_element_type=jnp.float32) + jnp.dot(
            far_rows, far_weight, preferred_element_type=jnp.float32
        )

    gate_proj = project(gate_pair)
    up_proj = project(up_pair)
    hidden = (jax.nn.silu(gate_proj) * up_proj).astype(jnp.bfloat16)
    hidden_all = lax.all_gather(hidden, "mlp", axis=0, tiled=False)
    unit = down_weight.shape[0] // mlp_count
    down_units = down_weight.reshape(mlp_count, unit, -1)
    partials = []
    for which in range(2):
        owners = [2 * which, 2 * which + 1, 2 * which + 4, 2 * which + 5]
        pieces_in = jnp.concatenate(
            [hidden_all[2 * which : 2 * which + 2], hidden_all[2 * which + 4 : 2 * which + 6]], 0
        )
        order = [unit_index for owner in owners for unit_index in (owner, owner ^ 2)]
        weight_in = down_units[jnp.array(order)].reshape(len(owners), 2 * unit, -1)
        partial = jnp.einsum(
            "dik,dkn->in", pieces_in, weight_in, preferred_element_type=jnp.float32
        )
        partials.append(partial.astype(jnp.bfloat16).reshape(req_count, row_half, -1))
    down_partial = jnp.concatenate(partials, 1).reshape(req_count * rows_here, -1)
    req_pieces = lax.all_to_all(down_partial, "req", 0, 0, tiled=True)
    feed = jnp.sum(
        req_pieces.reshape(req_count, rows_here, -1).astype(jnp.float32), axis=0
    )
    return (mixed_wide + feed).astype(jnp.bfloat16)


def solution(mesh):
    return jax.shard_map(
        per_device,
        mesh=mesh,
        in_specs=(
            P("req", "mlp"),
            P("req", "mlp"),
            P("req", "mlp"),
            P("req", "mlp"),
            P("req", None, "mlp"),
            P("req", None, "mlp"),
            P(None, "req", "mlp"),
            P(None, "req", "mlp"),
            P("req"),
            P("req"),
            P(),
            P(),
            P("mlp", None),
            P("mlp"),
            P(None, ("req", "mlp")),
            P(None, ("req", "mlp")),
            P("req", "mlp"),
        ),
        out_specs=P("req", "mlp"),
        check_vma=False,
    )
```

```python
import math

import jax
import jax.numpy as jnp
from jax import lax
from jax.sharding import PartitionSpec as P


D = 5120
HQ = 40
KV = 8
HD = 128


NEGATIVE = -1e30


def absorb(carried, scores, allowed, values, pattern):
    running, totals, summed = carried
    scores = jnp.where(allowed, scores, -jnp.inf)
    highest = jnp.maximum(running, jnp.max(scores, axis=-1))
    exponent = jnp.where(allowed, jnp.exp(scores - highest[..., None]), 0.0)
    fading = jnp.exp(running - highest)
    weights = exponent.astype(jnp.bfloat16)
    summed = summed * fading[..., None] + jnp.einsum(
        pattern, weights, values, preferred_element_type=jnp.float32
    )
    totals = totals * fading + jnp.sum(exponent, axis=-1)
    return (highest, totals, summed)


def per_device(
    resid,
    queries,
    new_keys,
    new_values,
    cache_keys,
    cache_values,
    context_keys,
    context_values,
    cache_lengths,
    group_ids,
    prefix_lengths,
    prompt_start,
    out_weight,
    norm_gain,
    gate_weight,
    up_weight,
    down_weight,
):
    rows_here = queries.shape[0]
    decode_count = cache_keys.shape[0]
    prompt_count = rows_here - decode_count
    heads_kv = new_keys.shape[1] // HD
    group_size = HQ // KV
    scaling = 1.0 / math.sqrt(HD)
    cache_span = cache_keys.shape[1]
    context_count = context_keys.shape[0]
    query_rows = queries.reshape(rows_here, heads_kv, group_size, HD)
    query_decode = query_rows[:decode_count]
    query_prompt = query_rows[decode_count:]
    key_rows = new_keys.reshape(rows_here, heads_kv, HD)
    value_rows = new_values.reshape(rows_here, heads_kv, HD)

    def fresh_state(row_count):
        return (
            jnp.full((row_count, heads_kv, group_size), NEGATIVE, jnp.float32),
            jnp.zeros((row_count, heads_kv, group_size), jnp.float32),
            jnp.zeros((row_count, heads_kv, group_size, HD), jnp.float32),
        )

    swap_with = [(i, i ^ 2) for i in range(lax.axis_size("mlp"))]
    gate_other = lax.ppermute(gate_weight, "mlp", swap_with)
    up_other = lax.ppermute(up_weight, "mlp", swap_with)
    past_keys = cache_keys.reshape(decode_count, cache_span, heads_kv, HD)
    past_values = cache_values.reshape(decode_count, cache_span, heads_kv, HD)
    scores = (
        jnp.einsum("ikgd,ickd->ikgc", query_decode, past_keys, preferred_element_type=jnp.float32)
        * scaling
    )
    usable = (jnp.arange(cache_span)[None, :] < cache_lengths[:, None])[:, None, None, :]
    decode_state = absorb(fresh_state(decode_count), scores, usable, past_values, "ikgc,ickd->ikgd")
    own_scores = (
        jnp.einsum(
            "ikgd,ikd->ikg",
            query_decode,
            key_rows[:decode_count],
            preferred_element_type=jnp.float32,
        )[..., None]
        * scaling
    )
    decode_state = absorb(
        decode_state,
        own_scores,
        jnp.ones(own_scores.shape, dtype=bool),
        value_rows[:decode_count][:, None],
        "ikgc,ickd->ikgd",
    )
    prompt_length = prompt_start[0]
    prefix_here = prefix_lengths[group_ids]
    state_decode = decode_state
    state_prompt = fresh_state(prompt_count)
    req_count = lax.axis_size("req")
    context_rows = context_keys.shape[1]
    packed = jnp.concatenate(
        [
            context_keys.reshape(context_count * context_rows, heads_kv * HD),
            context_values.reshape(context_count * context_rows, heads_kv * HD),
            new_keys,
            new_values,
        ],
        0,
    )
    gathered = lax.all_gather(packed, "req", axis=0, tiled=False)
    context_span = context_count * context_rows

    def context_of(offset):
        piece = gathered[:, offset : offset + context_span]
        piece = piece.reshape(req_count, context_count, context_rows, heads_kv * HD)
        return jnp.transpose(piece, (1, 0, 2, 3)).reshape(
            context_count, req_count * context_rows, heads_kv * HD
        )

    def prompt_of(offset):
        piece = gathered[:, offset : offset + rows_here][:, decode_count:]
        return piece.reshape(req_count * prompt_count, heads_kv * HD)

    key_block = context_of(0)
    value_block = context_of(context_span)
    extent = key_block.shape[1]
    positions = jnp.arange(extent)
    key_split = key_block.reshape(context_count, extent, heads_kv, HD)
    value_split = value_block.reshape(context_count, extent, heads_kv, HD)
    chosen_keys = key_split[group_ids]
    chosen_values = value_split[group_ids]
    block_scores = (
        jnp.einsum("ikgd,ickd->ikgc", query_decode, chosen_keys, preferred_element_type=jnp.float32)
        * scaling
    )
    block_usable = (positions[None, :] < prefix_here[:, None])[:, None, None, :]
    state_decode = absorb(
        state_decode, block_scores, block_usable, chosen_values, "ikgc,ickd->ikgd"
    )
    block_scores = (
        jnp.einsum(
            "jkgd,ckd->jkgc",
            query_prompt,
            key_split[context_count - 1],
            preferred_element_type=jnp.float32,
        )
        * scaling
    )
    block_usable = (positions < prompt_length)[None, None, None, :]
    state_prompt = absorb(
        state_prompt, block_scores, block_usable, value_split[context_count - 1], "jkgc,ckd->jkgd"
    )
    prompt_state = state_prompt
    own_positions = lax.axis_index("req") * prompt_count + jnp.arange(prompt_count, dtype=jnp.int32)
    key_block = prompt_of(2 * context_span)
    value_block = prompt_of(2 * context_span + rows_here)
    extent = key_block.shape[0]
    positions = jnp.arange(extent, dtype=jnp.int32)
    block_scores = (
        jnp.einsum(
            "jkgd,ckd->jkgc",
            query_prompt,
            key_block.reshape(extent, heads_kv, HD),
            preferred_element_type=jnp.float32,
        )
        * scaling
    )
    block_usable = (positions[None, :] <= own_positions[:, None])[:, None, None, :]
    prompt_state = absorb(
        prompt_state,
        block_scores,
        block_usable,
        value_block.reshape(extent, heads_kv, HD),
        "jkgc,ckd->jkgd",
    )

    def finish(carried):
        return (carried[2] / carried[1][..., None]).astype(jnp.bfloat16)

    attended = jnp.concatenate([finish(state_decode), finish(prompt_state)], 0).reshape(
        rows_here, heads_kv * group_size * HD
    )
    mlp_count = lax.axis_size("mlp")
    head_partial = jnp.dot(attended, out_weight, preferred_element_type=jnp.float32)
    pieces = lax.all_to_all(
        head_partial.astype(jnp.bfloat16), "mlp", 1, 0, tiled=True
    )
    projected = jnp.sum(
        pieces.reshape(mlp_count, rows_here, -1).astype(jnp.float32), axis=0
    )
    mixed = (resid.astype(jnp.float32) + projected).astype(jnp.bfloat16)
    mixed_wide = mixed.astype(jnp.float32)
    gain_pieces = []
    remainder = norm_gain
    for _ in range(3):
        piece = remainder.astype(jnp.bfloat16)
        gain_pieces.append(piece)
        remainder = remainder - piece.astype(jnp.float32)
    with_gain = jnp.concatenate([mixed, jnp.stack(gain_pieces, 0)], 0)
    gathered_rows = lax.all_gather(with_gain, "mlp", axis=1, tiled=True).astype(jnp.float32)
    mixed_rows = gathered_rows[:rows_here]
    full_gain = (gathered_rows[rows_here] + gathered_rows[rows_here + 1]) + gathered_rows[rows_here + 2]
    square_total = jnp.sum(mixed_rows * mixed_rows, axis=1)
    half = D // 2
    side = lax.axis_index("mlp") % 2
    own_half = lax.dynamic_slice_in_dim(mixed_rows, side * half, half, axis=1)
    own_gain = lax.dynamic_slice_in_dim(full_gain, side * half, half, axis=0)
    normed = (
        own_half * lax.rsqrt(square_total / D + 1e-06)[:, None] * own_gain[None, :]
    ).astype(jnp.bfloat16)
    pairs = [(i, i ^ 1) for i in range(mlp_count)]
    parity = (lax.axis_index("mlp") // 2) % 2
    gate_pair = jnp.concatenate([gate_weight, gate_other], 1)
    up_pair = jnp.concatenate([up_weight, up_other], 1)

    def halves(weight):
        return (
            lax.dynamic_slice_in_dim(weight, side * half, half, axis=0),
            lax.dynamic_slice_in_dim(weight, (1 - side) * half, half, axis=0),
        )

    row_half = rows_here // 2
    my_rows = lax.dynamic_slice_in_dim(normed, parity * row_half, row_half, axis=0)
    near_rows = lax.all_gather(my_rows, "req", axis=0, tiled=False)
    far_rows = lax.ppermute(near_rows, "mlp", pairs)

    def project(weight):
        near_weight, far_weight = halves(weight)
        return jnp.einsum(
            "rik,kn->rin", near_rows, near_weight, preferred_element_type=jnp.float32
        ) + jnp.einsum("rik,kn->rin", far_rows, far_weight, preferred_element_type=jnp.float32)

    gate_proj = project(gate_pair)
    up_proj = project(up_pair)
    hidden = (jax.nn.silu(gate_proj) * up_proj).astype(jnp.bfloat16)
    hidden_all = lax.all_gather(hidden, "mlp", axis=0, tiled=False)
    unit = down_weight.shape[0] // mlp_count
    hidden_all = hidden_all.reshape(2, 2, 2, req_count, row_half, 2 * unit)
    down_units = down_weight.reshape(2, 2, 2, unit, -1)
    down_units = jnp.transpose(down_units, (0, 2, 1, 3, 4))
    down_stack = jnp.stack(
        [
            down_units.reshape(2, 2, 2 * unit, -1),
            down_units[:, :, ::-1].reshape(2, 2, 2 * unit, -1),
        ],
        0,
    )
    down_partial = jnp.einsum(
        "aqcrik,qacko->rqio", hidden_all, down_stack, preferred_element_type=jnp.float32
    ).astype(jnp.bfloat16)
    req_pieces = lax.all_to_all(
        down_partial.reshape(req_count * rows_here, -1), "req", 0, 0, tiled=True
    )
    feed = jnp.sum(
        req_pieces.reshape(req_count, rows_here, -1).astype(jnp.float32), axis=0
    )
    return (mixed_wide + feed).astype(jnp.bfloat16)


def solution(mesh):
    return jax.shard_map(
        per_device,
        mesh=mesh,
        in_specs=(
            P("req", "mlp"),
            P("req", "mlp"),
            P("req", "mlp"),
            P("req", "mlp"),
            P("req", None, "mlp"),
            P("req", None, "mlp"),
            P(None, "req", "mlp"),
            P(None, "req", "mlp"),
            P("req"),
            P("req"),
            P(),
            P(),
            P("mlp", None),
            P("mlp"),
            P(None, ("req", "mlp")),
            P(None, ("req", "mlp")),
            P("req", "mlp"),
        ),
        out_specs=P("req", "mlp"),
        check_vma=False,
    )
```

```python
import math

import jax
import jax.numpy as jnp
from jax import lax
from jax.sharding import PartitionSpec as P

D = 5120
HQ = 40
KV = 8
HD = 128


NEGATIVE = -1e30


def absorb(carried, scores, allowed, values, pattern):
    running, totals, summed = carried
    scores = jnp.where(allowed, scores, -jnp.inf)
    highest = jnp.maximum(running, jnp.max(scores, axis=-1))
    exponent = jnp.where(allowed, jnp.exp(scores - highest[..., None]), 0.0)
    fading = jnp.exp(running - highest)
    weights = exponent.astype(jnp.bfloat16)
    summed = summed * fading[..., None] + jnp.einsum(
        pattern, weights, values, preferred_element_type=jnp.float32
    )
    totals = totals * fading + jnp.sum(exponent, axis=-1)
    return (highest, totals, summed)


def per_device(
    resid,
    queries,
    new_keys,
    new_values,
    cache_keys,
    cache_values,
    context_keys,
    context_values,
    cache_lengths,
    group_ids,
    prefix_lengths,
    prompt_start,
    out_weight,
    norm_gain,
    gate_weight,
    up_weight,
    down_weight,
):
    rows_here = queries.shape[0]
    decode_count = cache_keys.shape[0]
    prompt_count = rows_here - decode_count
    heads_kv = new_keys.shape[1] // HD
    group_size = HQ // KV
    scaling = 1.0 / math.sqrt(HD)
    cache_span = cache_keys.shape[1]
    context_count = context_keys.shape[0]
    query_rows = queries.reshape(rows_here, heads_kv, group_size, HD)
    query_decode = query_rows[:decode_count]
    query_prompt = query_rows[decode_count:]
    key_rows = new_keys.reshape(rows_here, heads_kv, HD)
    value_rows = new_values.reshape(rows_here, heads_kv, HD)

    def fresh_state(row_count):
        return (
            jnp.full((row_count, heads_kv, group_size), NEGATIVE, jnp.float32),
            jnp.zeros((row_count, heads_kv, group_size), jnp.float32),
            jnp.zeros((row_count, heads_kv, group_size, HD), jnp.float32),
        )

    past_keys = cache_keys.reshape(decode_count, cache_span, heads_kv, HD)
    past_values = cache_values.reshape(decode_count, cache_span, heads_kv, HD)
    scores = (
        jnp.einsum("ikgd,ickd->ikgc", query_decode, past_keys, preferred_element_type=jnp.float32)
        * scaling
    )
    usable = (jnp.arange(cache_span)[None, :] < cache_lengths[:, None])[:, None, None, :]
    decode_state = absorb(fresh_state(decode_count), scores, usable, past_values, "ikgc,ickd->ikgd")
    own_scores = (
        jnp.einsum(
            "ikgd,ikd->ikg",
            query_decode,
            key_rows[:decode_count],
            preferred_element_type=jnp.float32,
        )[..., None]
        * scaling
    )
    decode_state = absorb(
        decode_state,
        own_scores,
        jnp.ones(own_scores.shape, dtype=bool),
        value_rows[:decode_count][:, None],
        "ikgc,ickd->ikgd",
    )
    prompt_length = prompt_start[0]
    prefix_here = prefix_lengths[group_ids]
    state_decode = decode_state
    state_prompt = fresh_state(prompt_count)
    req_count = lax.axis_size("req")
    context_rows = context_keys.shape[1]
    context_pack = jnp.concatenate(
        [
            context_keys.reshape(context_count * context_rows, heads_kv * HD),
            context_values.reshape(context_count * context_rows, heads_kv * HD),
        ],
        0,
    )
    context_gathered = lax.all_gather(context_pack, "req", axis=0, tiled=False)
    new_pack = jnp.concatenate([new_keys, new_values], 0)
    new_copies = jnp.broadcast_to(new_pack[None], (req_count,) + new_pack.shape)
    new_gathered = lax.all_to_all(
        new_copies.reshape(req_count * new_pack.shape[0], -1), "req", 0, 0, tiled=True
    ).reshape(req_count, new_pack.shape[0], -1)
    context_span = context_count * context_rows

    def context_of(offset):
        piece = context_gathered[:, offset : offset + context_span]
        piece = piece.reshape(req_count, context_count, context_rows, heads_kv * HD)
        return jnp.transpose(piece, (1, 0, 2, 3)).reshape(
            context_count, req_count * context_rows, heads_kv * HD
        )

    def prompt_of(offset):
        piece = new_gathered[:, offset : offset + rows_here][:, decode_count:]
        return piece.reshape(req_count * prompt_count, heads_kv * HD)

    key_block = context_of(0)
    value_block = context_of(context_span)
    extent = key_block.shape[1]
    positions = jnp.arange(extent)
    key_split = key_block.reshape(context_count, extent, heads_kv, HD)
    value_split = value_block.reshape(context_count, extent, heads_kv, HD)
    chosen_keys = key_split[group_ids]
    chosen_values = value_split[group_ids]
    block_scores = (
        jnp.einsum("ikgd,ickd->ikgc", query_decode, chosen_keys, preferred_element_type=jnp.float32)
        * scaling
    )
    block_usable = (positions[None, :] < prefix_here[:, None])[:, None, None, :]
    state_decode = absorb(
        state_decode, block_scores, block_usable, chosen_values, "ikgc,ickd->ikgd"
    )
    block_scores = (
        jnp.einsum(
            "jkgd,ckd->jkgc",
            query_prompt,
            key_split[context_count - 1],
            preferred_element_type=jnp.float32,
        )
        * scaling
    )
    block_usable = (positions < prompt_length)[None, None, None, :]
    state_prompt = absorb(
        state_prompt, block_scores, block_usable, value_split[context_count - 1], "jkgc,ckd->jkgd"
    )
    prompt_state = state_prompt
    own_positions = lax.axis_index("req") * prompt_count + jnp.arange(prompt_count, dtype=jnp.int32)
    key_block = prompt_of(0)
    value_block = prompt_of(rows_here)
    extent = key_block.shape[0]
    positions = jnp.arange(extent, dtype=jnp.int32)
    block_scores = (
        jnp.einsum(
            "jkgd,ckd->jkgc",
            query_prompt,
            key_block.reshape(extent, heads_kv, HD),
            preferred_element_type=jnp.float32,
        )
        * scaling
    )
    block_usable = (positions[None, :] <= own_positions[:, None])[:, None, None, :]
    prompt_state = absorb(
        prompt_state,
        block_scores,
        block_usable,
        value_block.reshape(extent, heads_kv, HD),
        "jkgc,ckd->jkgd",
    )

    def finish(carried):
        return (carried[2] / carried[1][..., None]).astype(jnp.bfloat16)

    attended = jnp.concatenate([finish(state_decode), finish(prompt_state)], 0).reshape(
        rows_here, heads_kv * group_size * HD
    )
    mlp_count = lax.axis_size("mlp")
    head_partial = jnp.dot(attended, out_weight, preferred_element_type=jnp.float32)
    pieces = lax.all_to_all(
        head_partial.astype(jnp.bfloat16), "mlp", 1, 0, tiled=True
    )
    projected = jnp.sum(
        pieces.reshape(mlp_count, rows_here, -1).astype(jnp.float32), axis=0
    )
    mixed = (resid.astype(jnp.float32) + projected).astype(jnp.bfloat16)
    mixed_wide = mixed.astype(jnp.float32)
    mixed_rows = lax.all_gather(mixed, "mlp", axis=1, tiled=True).astype(jnp.float32)
    square_total = jnp.sum(mixed_rows * mixed_rows, axis=1)
    half = D // 2
    side = lax.axis_index("mlp") % 2
    own_half = lax.dynamic_slice_in_dim(mixed_rows, side * half, half, axis=1)
    own_gain = lax.dynamic_slice_in_dim(norm_gain, side * half, half, axis=0)
    normed = (
        own_half * lax.rsqrt(square_total / D + 1e-06)[:, None] * own_gain[None, :]
    ).astype(jnp.bfloat16)
    near_rows = lax.all_gather(normed, "req", axis=0, tiled=True)
    pairs = [(i, i ^ 1) for i in range(mlp_count)]
    far_rows = lax.ppermute(near_rows, "mlp", pairs)

    def project(weight):
        near_weight = lax.dynamic_slice_in_dim(weight, side * half, half, axis=0)
        far_weight = lax.dynamic_slice_in_dim(weight, (1 - side) * half, half, axis=0)
        return jnp.dot(near_rows, near_weight, preferred_element_type=jnp.float32) + jnp.dot(
            far_rows, far_weight, preferred_element_type=jnp.float32
        )

    gate_proj = project(gate_weight)
    up_proj = project(up_weight)
    hidden = (jax.nn.silu(gate_proj) * up_proj).astype(jnp.bfloat16)
    hidden_block = lax.all_gather(hidden, "mlp", axis=1, tiled=True)
    down_partial = jnp.dot(hidden_block, down_weight, preferred_element_type=jnp.float32)
    req_pieces = lax.all_to_all(down_partial.astype(jnp.bfloat16), "req", 0, 0, tiled=True)
    feed = jnp.sum(
        req_pieces.reshape(req_count, rows_here, -1).astype(jnp.float32), axis=0
    )
    return (mixed_wide + feed).astype(jnp.bfloat16)


def solution(mesh):
    return jax.shard_map(
        per_device,
        mesh=mesh,
        in_specs=(
            P("req", "mlp"),
            P("req", "mlp"),
            P("req", "mlp"),
            P("req", "mlp"),
            P("req", None, "mlp"),
            P("req", None, "mlp"),
            P(None, "req", "mlp"),
            P(None, "req", "mlp"),
            P("req"),
            P("req"),
            P(),
            P(),
            P("mlp", None),
            P(),
            P(None, ("req", "mlp")),
            P(None, ("req", "mlp")),
            P("req", "mlp"),
        ),
        out_specs=P("req", "mlp"),
        check_vma=False,
    )
```

```python
import math

import jax
import jax.numpy as jnp
from jax import lax
from jax.sharding import PartitionSpec as P


D = 5120
HQ = 40
KV = 8
HD = 128


NEGATIVE = -1e30


def absorb(carried, scores, allowed, values, pattern):
    running, totals, summed = carried
    scores = jnp.where(allowed, scores, -jnp.inf)
    highest = jnp.maximum(running, jnp.max(scores, axis=-1))
    exponent = jnp.where(allowed, jnp.exp(scores - highest[..., None]), 0.0)
    fading = jnp.exp(running - highest)
    weights = exponent.astype(jnp.bfloat16)
    summed = summed * fading[..., None] + jnp.einsum(
        pattern, weights, values, preferred_element_type=jnp.float32
    )
    totals = totals * fading + jnp.sum(exponent, axis=-1)
    return (highest, totals, summed)


def per_device(
    resid,
    queries,
    new_keys,
    new_values,
    cache_keys,
    cache_values,
    context_keys,
    context_values,
    cache_lengths,
    group_ids,
    prefix_lengths,
    prompt_start,
    out_weight,
    norm_gain,
    gate_weight,
    up_weight,
    down_weight,
):
    rows_here = queries.shape[0]
    decode_count = cache_keys.shape[0]
    prompt_count = rows_here - decode_count
    heads_kv = new_keys.shape[1] // HD
    group_size = HQ // KV
    scaling = 1.0 / math.sqrt(HD)
    cache_span = cache_keys.shape[1]
    context_count = context_keys.shape[0]
    query_rows = queries.reshape(rows_here, heads_kv, group_size, HD)
    query_decode = query_rows[:decode_count]
    query_prompt = query_rows[decode_count:]
    key_rows = new_keys.reshape(rows_here, heads_kv, HD)
    value_rows = new_values.reshape(rows_here, heads_kv, HD)

    def fresh_state(row_count):
        return (
            jnp.full((row_count, heads_kv, group_size), NEGATIVE, jnp.float32),
            jnp.zeros((row_count, heads_kv, group_size), jnp.float32),
            jnp.zeros((row_count, heads_kv, group_size, HD), jnp.float32),
        )

    swap_with = [(i, i ^ 2) for i in range(lax.axis_size("mlp"))]
    gate_other = lax.ppermute(gate_weight, "mlp", swap_with)
    up_other = lax.ppermute(up_weight, "mlp", swap_with)
    past_keys = cache_keys.reshape(decode_count, cache_span, heads_kv, HD)
    past_values = cache_values.reshape(decode_count, cache_span, heads_kv, HD)
    scores = (
        jnp.einsum("ikgd,ickd->ikgc", query_decode, past_keys, preferred_element_type=jnp.float32)
        * scaling
    )
    usable = (jnp.arange(cache_span)[None, :] < cache_lengths[:, None])[:, None, None, :]
    decode_state = absorb(fresh_state(decode_count), scores, usable, past_values, "ikgc,ickd->ikgd")
    own_scores = (
        jnp.einsum(
            "ikgd,ikd->ikg",
            query_decode,
            key_rows[:decode_count],
            preferred_element_type=jnp.float32,
        )[..., None]
        * scaling
    )
    decode_state = absorb(
        decode_state,
        own_scores,
        jnp.ones(own_scores.shape, dtype=bool),
        value_rows[:decode_count][:, None],
        "ikgc,ickd->ikgd",
    )
    prompt_length = prompt_start[0]
    prefix_here = prefix_lengths[group_ids]
    state_decode = decode_state
    state_prompt = fresh_state(prompt_count)
    req_count = lax.axis_size("req")
    context_rows = context_keys.shape[1]
    packed = jnp.concatenate(
        [
            context_keys.reshape(context_count * context_rows, heads_kv * HD),
            context_values.reshape(context_count * context_rows, heads_kv * HD),
            new_keys,
            new_values,
        ],
        0,
    )
    gathered = lax.all_gather(packed, "req", axis=0, tiled=False)
    context_span = context_count * context_rows

    def context_of(offset):
        piece = gathered[:, offset : offset + context_span]
        piece = piece.reshape(req_count, context_count, context_rows, heads_kv * HD)
        return jnp.transpose(piece, (1, 0, 2, 3)).reshape(
            context_count, req_count * context_rows, heads_kv * HD
        )

    def prompt_of(offset):
        piece = gathered[:, offset : offset + rows_here][:, decode_count:]
        return piece.reshape(req_count * prompt_count, heads_kv * HD)

    key_block = context_of(0)
    value_block = context_of(context_span)
    extent = key_block.shape[1]
    positions = jnp.arange(extent)
    key_split = key_block.reshape(context_count, extent, heads_kv, HD)
    value_split = value_block.reshape(context_count, extent, heads_kv, HD)
    chosen_keys = key_split[group_ids]
    chosen_values = value_split[group_ids]
    block_scores = (
        jnp.einsum("ikgd,ickd->ikgc", query_decode, chosen_keys, preferred_element_type=jnp.float32)
        * scaling
    )
    block_usable = (positions[None, :] < prefix_here[:, None])[:, None, None, :]
    state_decode = absorb(
        state_decode, block_scores, block_usable, chosen_values, "ikgc,ickd->ikgd"
    )
    block_scores = (
        jnp.einsum(
            "jkgd,ckd->jkgc",
            query_prompt,
            key_split[context_count - 1],
            preferred_element_type=jnp.float32,
        )
        * scaling
    )
    block_usable = (positions < prompt_length)[None, None, None, :]
    state_prompt = absorb(
        state_prompt, block_scores, block_usable, value_split[context_count - 1], "jkgc,ckd->jkgd"
    )
    prompt_state = state_prompt
    own_positions = lax.axis_index("req") * prompt_count + jnp.arange(prompt_count, dtype=jnp.int32)
    key_block = prompt_of(2 * context_span)
    value_block = prompt_of(2 * context_span + rows_here)
    extent = key_block.shape[0]
    positions = jnp.arange(extent, dtype=jnp.int32)
    block_scores = (
        jnp.einsum(
            "jkgd,ckd->jkgc",
            query_prompt,
            key_block.reshape(extent, heads_kv, HD),
            preferred_element_type=jnp.float32,
        )
        * scaling
    )
    block_usable = (positions[None, :] <= own_positions[:, None])[:, None, None, :]
    prompt_state = absorb(
        prompt_state,
        block_scores,
        block_usable,
        value_block.reshape(extent, heads_kv, HD),
        "jkgc,ckd->jkgd",
    )

    def finish(carried):
        return (carried[2] / carried[1][..., None]).astype(jnp.bfloat16)

    attended = jnp.concatenate([finish(state_decode), finish(prompt_state)], 0).reshape(
        rows_here, heads_kv * group_size * HD
    )
    mlp_count = lax.axis_size("mlp")
    head_partial = jnp.dot(attended, out_weight, preferred_element_type=jnp.float32)
    pieces = lax.all_to_all(
        head_partial.astype(jnp.bfloat16), "mlp", 1, 0, tiled=True
    )
    projected = jnp.sum(
        pieces.reshape(mlp_count, rows_here, -1).astype(jnp.float32), axis=0
    )
    mixed = (resid.astype(jnp.float32) + projected).astype(jnp.bfloat16)
    mixed_wide = mixed.astype(jnp.float32)
    gain_pieces = []
    remainder = norm_gain
    for _ in range(3):
        piece = remainder.astype(jnp.bfloat16)
        gain_pieces.append(piece)
        remainder = remainder - piece.astype(jnp.float32)
    with_gain = jnp.concatenate([mixed, jnp.stack(gain_pieces, 0)], 0)
    gathered_rows = lax.all_gather(with_gain, "mlp", axis=1, tiled=True).astype(jnp.float32)
    mixed_rows = gathered_rows[:rows_here]
    full_gain = (gathered_rows[rows_here] + gathered_rows[rows_here + 1]) + gathered_rows[rows_here + 2]
    square_total = jnp.sum(mixed_rows * mixed_rows, axis=1)
    half = D // 2
    side = lax.axis_index("mlp") % 2
    own_half = lax.dynamic_slice_in_dim(mixed_rows, side * half, half, axis=1)
    own_gain = lax.dynamic_slice_in_dim(full_gain, side * half, half, axis=0)
    normed = (
        own_half * lax.rsqrt(square_total / D + 1e-06)[:, None] * own_gain[None, :]
    ).astype(jnp.bfloat16)
    pairs = [(i, i ^ 1) for i in range(mlp_count)]
    parity = (lax.axis_index("mlp") // 2) % 2

    def halves(weight):
        return (
            lax.dynamic_slice_in_dim(weight, side * half, half, axis=0),
            lax.dynamic_slice_in_dim(weight, (1 - side) * half, half, axis=0),
        )

    row_half = rows_here // 2
    my_rows = lax.dynamic_slice_in_dim(normed, parity * row_half, row_half, axis=0)
    near_rows = lax.all_gather(my_rows, "req", axis=1, tiled=True)
    far_rows = lax.ppermute(near_rows, "mlp", pairs)
    near_split = near_rows.reshape(row_half, req_count, half)
    far_split = far_rows.reshape(row_half, req_count, half)

    def project(weight):
        near_weight, far_weight = halves(weight)
        return jnp.einsum(
            "irk,kn->irn", near_split, near_weight, preferred_element_type=jnp.float32
        ) + jnp.einsum("irk,kn->irn", far_split, far_weight, preferred_element_type=jnp.float32)

    def activate(gate_part, up_part):
        return (jax.nn.silu(project(gate_part)) * project(up_part)).astype(jnp.bfloat16)

    hidden = jnp.stack([activate(gate_weight, up_weight), activate(gate_other, up_other)], 2)
    hidden_all = lax.all_gather(hidden, "mlp", axis=0, tiled=False)
    unit = down_weight.shape[0] // mlp_count
    hidden_all = hidden_all.reshape(2, 2, 2, row_half, req_count, 2, unit)
    by_parity = jnp.stack([hidden_all[:, 0], hidden_all[:, 1, :, :, :, ::-1]], 0)
    hidden_block = jnp.transpose(by_parity, (4, 0, 3, 1, 5, 2, 6)).reshape(
        req_count * rows_here, mlp_count * unit
    )
    down_partial = jnp.dot(hidden_block, down_weight, preferred_element_type=jnp.float32)
    req_pieces = lax.all_to_all(down_partial.astype(jnp.bfloat16), "req", 0, 0, tiled=True)
    feed = jnp.sum(
        req_pieces.reshape(req_count, rows_here, -1).astype(jnp.float32), axis=0
    )
    return (mixed_wide + feed).astype(jnp.bfloat16)


def solution(mesh):
    return jax.shard_map(
        per_device,
        mesh=mesh,
        in_specs=(
            P("req", "mlp"),
            P("req", "mlp"),
            P("req", "mlp"),
            P("req", "mlp"),
            P("req", None, "mlp"),
            P("req", None, "mlp"),
            P(None, "req", "mlp"),
            P(None, "req", "mlp"),
            P("req"),
            P("req"),
            P(),
            P(),
            P("mlp", None),
            P("mlp"),
            P(None, ("req", "mlp")),
            P(None, ("req", "mlp")),
            P("req", "mlp"),
        ),
        out_specs=P("req", "mlp"),
        check_vma=False,
    )
```

```python
import math

import jax
import jax.numpy as jnp
from jax import lax
from jax.sharding import PartitionSpec as P


D = 5120
HQ = 40
KV = 8
HD = 128


NEGATIVE = -1e30


def absorb(carried, scores, allowed, values, pattern):
    running, totals, summed = carried
    scores = jnp.where(allowed, scores, -jnp.inf)
    highest = jnp.maximum(running, jnp.max(scores, axis=-1))
    exponent = jnp.where(allowed, jnp.exp(scores - highest[..., None]), 0.0)
    fading = jnp.exp(running - highest)
    weights = exponent.astype(jnp.bfloat16)
    summed = summed * fading[..., None] + jnp.einsum(
        pattern, weights, values, preferred_element_type=jnp.float32
    )
    totals = totals * fading + jnp.sum(exponent, axis=-1)
    return (highest, totals, summed)


def per_device(
    resid,
    queries,
    new_keys,
    new_values,
    cache_keys,
    cache_values,
    context_keys,
    context_values,
    cache_lengths,
    group_ids,
    prefix_lengths,
    prompt_start,
    out_weight,
    norm_gain,
    gate_weight,
    up_weight,
    down_weight,
):
    rows_here = queries.shape[0]
    decode_count = cache_keys.shape[0]
    prompt_count = rows_here - decode_count
    heads_kv = new_keys.shape[1] // HD
    group_size = HQ // KV
    scaling = 1.0 / math.sqrt(HD)
    cache_span = cache_keys.shape[1]
    context_count = context_keys.shape[0]
    query_rows = queries.reshape(rows_here, heads_kv, group_size, HD)
    query_decode = query_rows[:decode_count]
    query_prompt = query_rows[decode_count:]
    key_rows = new_keys.reshape(rows_here, heads_kv, HD)
    value_rows = new_values.reshape(rows_here, heads_kv, HD)

    def fresh_state(row_count):
        return (
            jnp.full((row_count, heads_kv, group_size), NEGATIVE, jnp.float32),
            jnp.zeros((row_count, heads_kv, group_size), jnp.float32),
            jnp.zeros((row_count, heads_kv, group_size, HD), jnp.float32),
        )

    swap_with = [(i, i ^ 2) for i in range(lax.axis_size("mlp"))]
    gate_other = lax.ppermute(gate_weight, "mlp", swap_with)
    up_other = lax.ppermute(up_weight, "mlp", swap_with)
    past_keys = cache_keys.reshape(decode_count, cache_span, heads_kv, HD)
    past_values = cache_values.reshape(decode_count, cache_span, heads_kv, HD)
    scores = (
        jnp.einsum("ikgd,ickd->ikgc", query_decode, past_keys, preferred_element_type=jnp.float32)
        * scaling
    )
    usable = (jnp.arange(cache_span)[None, :] < cache_lengths[:, None])[:, None, None, :]
    decode_state = absorb(fresh_state(decode_count), scores, usable, past_values, "ikgc,ickd->ikgd")
    own_scores = (
        jnp.einsum(
            "ikgd,ikd->ikg",
            query_decode,
            key_rows[:decode_count],
            preferred_element_type=jnp.float32,
        )[..., None]
        * scaling
    )
    decode_state = absorb(
        decode_state,
        own_scores,
        jnp.ones(own_scores.shape, dtype=bool),
        value_rows[:decode_count][:, None],
        "ikgc,ickd->ikgd",
    )
    prompt_length = prompt_start[0]
    prefix_here = prefix_lengths[group_ids]
    state_decode = decode_state
    state_prompt = fresh_state(prompt_count)
    req_count = lax.axis_size("req")
    context_rows = context_keys.shape[1]
    packed = jnp.concatenate(
        [
            context_keys.reshape(context_count * context_rows, heads_kv * HD),
            context_values.reshape(context_count * context_rows, heads_kv * HD),
            new_keys,
            new_values,
        ],
        0,
    )
    gathered = lax.all_gather(packed, "req", axis=0, tiled=False)
    context_span = context_count * context_rows

    def context_of(offset):
        piece = gathered[:, offset : offset + context_span]
        piece = piece.reshape(req_count, context_count, context_rows, heads_kv * HD)
        return jnp.transpose(piece, (1, 0, 2, 3)).reshape(
            context_count, req_count * context_rows, heads_kv * HD
        )

    def prompt_of(offset):
        piece = gathered[:, offset : offset + rows_here][:, decode_count:]
        return piece.reshape(req_count * prompt_count, heads_kv * HD)

    key_block = context_of(0)
    value_block = context_of(context_span)
    extent = key_block.shape[1]
    positions = jnp.arange(extent)
    key_split = key_block.reshape(context_count, extent, heads_kv, HD)
    value_split = value_block.reshape(context_count, extent, heads_kv, HD)
    chosen_keys = key_split[group_ids]
    chosen_values = value_split[group_ids]
    block_scores = (
        jnp.einsum("ikgd,ickd->ikgc", query_decode, chosen_keys, preferred_element_type=jnp.float32)
        * scaling
    )
    block_usable = (positions[None, :] < prefix_here[:, None])[:, None, None, :]
    state_decode = absorb(
        state_decode, block_scores, block_usable, chosen_values, "ikgc,ickd->ikgd"
    )
    block_scores = (
        jnp.einsum(
            "jkgd,ckd->jkgc",
            query_prompt,
            key_split[context_count - 1],
            preferred_element_type=jnp.float32,
        )
        * scaling
    )
    block_usable = (positions < prompt_length)[None, None, None, :]
    state_prompt = absorb(
        state_prompt, block_scores, block_usable, value_split[context_count - 1], "jkgc,ckd->jkgd"
    )
    prompt_state = state_prompt
    own_positions = lax.axis_index("req") * prompt_count + jnp.arange(prompt_count, dtype=jnp.int32)
    key_block = prompt_of(2 * context_span)
    value_block = prompt_of(2 * context_span + rows_here)
    extent = key_block.shape[0]
    positions = jnp.arange(extent, dtype=jnp.int32)
    block_scores = (
        jnp.einsum(
            "jkgd,ckd->jkgc",
            query_prompt,
            key_block.reshape(extent, heads_kv, HD),
            preferred_element_type=jnp.float32,
        )
        * scaling
    )
    block_usable = (positions[None, :] <= own_positions[:, None])[:, None, None, :]
    prompt_state = absorb(
        prompt_state,
        block_scores,
        block_usable,
        value_block.reshape(extent, heads_kv, HD),
        "jkgc,ckd->jkgd",
    )

    def finish(carried):
        return (carried[2] / carried[1][..., None]).astype(jnp.bfloat16)

    attended = jnp.concatenate([finish(state_decode), finish(prompt_state)], 0).reshape(
        rows_here, heads_kv * group_size * HD
    )
    mlp_count = lax.axis_size("mlp")
    head_partial = jnp.dot(attended, out_weight, preferred_element_type=jnp.float32)
    pieces = lax.all_to_all(
        head_partial.astype(jnp.bfloat16), "mlp", 1, 0, tiled=True
    )
    projected = jnp.sum(
        pieces.reshape(mlp_count, rows_here, -1).astype(jnp.float32), axis=0
    )
    mixed = (resid.astype(jnp.float32) + projected).astype(jnp.bfloat16)
    mixed_wide = mixed.astype(jnp.float32)
    gain_pieces = []
    remainder = norm_gain
    for _ in range(3):
        piece = remainder.astype(jnp.bfloat16)
        gain_pieces.append(piece)
        remainder = remainder - piece.astype(jnp.float32)
    with_gain = jnp.concatenate([mixed, jnp.stack(gain_pieces, 0)], 0)
    gathered_rows = lax.all_gather(with_gain, "mlp", axis=1, tiled=True).astype(jnp.float32)
    mixed_rows = gathered_rows[:rows_here]
    full_gain = (gathered_rows[rows_here] + gathered_rows[rows_here + 1]) + gathered_rows[rows_here + 2]
    square_total = jnp.sum(mixed_rows * mixed_rows, axis=1)
    half = D // 2
    side = lax.axis_index("mlp") % 2
    own_half = lax.dynamic_slice_in_dim(mixed_rows, side * half, half, axis=1)
    own_gain = lax.dynamic_slice_in_dim(full_gain, side * half, half, axis=0)
    normed = (
        own_half * lax.rsqrt(square_total / D + 1e-06)[:, None] * own_gain[None, :]
    ).astype(jnp.bfloat16)
    pairs = [(i, i ^ 1) for i in range(mlp_count)]
    parity = (lax.axis_index("mlp") // 2) % 2

    def halves(weight):
        return (
            lax.dynamic_slice_in_dim(weight, side * half, half, axis=0),
            lax.dynamic_slice_in_dim(weight, (1 - side) * half, half, axis=0),
        )

    row_half = rows_here // 2
    my_rows = lax.dynamic_slice_in_dim(normed, parity * row_half, row_half, axis=0)
    near_rows = lax.all_gather(my_rows, "req", axis=0, tiled=True)
    far_rows = lax.ppermute(near_rows, "mlp", pairs)

    def project(weight):
        near_weight, far_weight = halves(weight)
        return jnp.dot(near_rows, near_weight, preferred_element_type=jnp.float32) + jnp.dot(
            far_rows, far_weight, preferred_element_type=jnp.float32
        )

    def activate(gate_part, up_part):
        return (jax.nn.silu(project(gate_part)) * project(up_part)).astype(jnp.bfloat16)

    hidden = jnp.concatenate(
        [activate(gate_weight, up_weight), activate(gate_other, up_other)], 1
    )
    hidden_all = lax.all_gather(hidden, "mlp", axis=0, tiled=False)
    unit = down_weight.shape[0] // mlp_count
    down_units = down_weight.reshape(mlp_count, unit, -1)
    sums = [None, None]
    for owner in range(mlp_count):
        which = (owner // 2) % 2
        block = jnp.concatenate([down_units[owner], down_units[owner ^ 2]], 0)
        term = jnp.dot(hidden_all[owner], block, preferred_element_type=jnp.float32)
        sums[which] = term if sums[which] is None else sums[which] + term
    down_partial = jnp.stack(
        [total.reshape(req_count, row_half, -1) for total in sums], 1
    ).astype(jnp.bfloat16)
    req_pieces = lax.all_to_all(
        down_partial.reshape(req_count * rows_here, -1), "req", 0, 0, tiled=True
    )
    feed = jnp.sum(
        req_pieces.reshape(req_count, rows_here, -1).astype(jnp.float32), axis=0
    )
    return (mixed_wide + feed).astype(jnp.bfloat16)


def solution(mesh):
    return jax.shard_map(
        per_device,
        mesh=mesh,
        in_specs=(
            P("req", "mlp"),
            P("req", "mlp"),
            P("req", "mlp"),
            P("req", "mlp"),
            P("req", None, "mlp"),
            P("req", None, "mlp"),
            P(None, "req", "mlp"),
            P(None, "req", "mlp"),
            P("req"),
            P("req"),
            P(),
            P(),
            P("mlp", None),
            P("mlp"),
            P(None, ("req", "mlp")),
            P(None, ("req", "mlp")),
            P("req", "mlp"),
        ),
        out_specs=P("req", "mlp"),
        check_vma=False,
    )
```

```python
import math

import jax
import jax.numpy as jnp
from jax import lax
from jax.sharding import PartitionSpec as P

D = 5120
HQ = 40
KV = 8
HD = 128


NEGATIVE = -1e30


def absorb(carried, scores, allowed, values, pattern):
    running, totals, summed = carried
    scores = jnp.where(allowed, scores, -jnp.inf)
    highest = jnp.maximum(running, jnp.max(scores, axis=-1))
    exponent = jnp.where(allowed, jnp.exp(scores - highest[..., None]), 0.0)
    fading = jnp.exp(running - highest)
    weights = exponent.astype(jnp.bfloat16)
    summed = summed * fading[..., None] + jnp.einsum(
        pattern, weights, values, preferred_element_type=jnp.float32
    )
    totals = totals * fading + jnp.sum(exponent, axis=-1)
    return (highest, totals, summed)


def per_device(
    resid,
    queries,
    new_keys,
    new_values,
    cache_keys,
    cache_values,
    context_keys,
    context_values,
    cache_lengths,
    group_ids,
    prefix_lengths,
    prompt_start,
    out_weight,
    norm_gain,
    gate_weight,
    up_weight,
    down_weight,
):
    rows_here = queries.shape[0]
    decode_count = cache_keys.shape[0]
    prompt_count = rows_here - decode_count
    heads_kv = new_keys.shape[1] // HD
    group_size = HQ // KV
    scaling = 1.0 / math.sqrt(HD)
    cache_span = cache_keys.shape[1]
    context_count = context_keys.shape[0]
    query_rows = queries.reshape(rows_here, heads_kv, group_size, HD)
    query_decode = query_rows[:decode_count]
    query_prompt = query_rows[decode_count:]
    key_rows = new_keys.reshape(rows_here, heads_kv, HD)
    value_rows = new_values.reshape(rows_here, heads_kv, HD)

    def fresh_state(row_count):
        return (
            jnp.full((row_count, heads_kv, group_size), NEGATIVE, jnp.float32),
            jnp.zeros((row_count, heads_kv, group_size), jnp.float32),
            jnp.zeros((row_count, heads_kv, group_size, HD), jnp.float32),
        )

    past_keys = cache_keys.reshape(decode_count, cache_span, heads_kv, HD)
    past_values = cache_values.reshape(decode_count, cache_span, heads_kv, HD)
    scores = (
        jnp.einsum("ikgd,ickd->ikgc", query_decode, past_keys, preferred_element_type=jnp.float32)
        * scaling
    )
    usable = (jnp.arange(cache_span)[None, :] < cache_lengths[:, None])[:, None, None, :]
    decode_state = absorb(fresh_state(decode_count), scores, usable, past_values, "ikgc,ickd->ikgd")
    own_scores = (
        jnp.einsum(
            "ikgd,ikd->ikg",
            query_decode,
            key_rows[:decode_count],
            preferred_element_type=jnp.float32,
        )[..., None]
        * scaling
    )
    decode_state = absorb(
        decode_state,
        own_scores,
        jnp.ones(own_scores.shape, dtype=bool),
        value_rows[:decode_count][:, None],
        "ikgc,ickd->ikgd",
    )
    prompt_length = prompt_start[0]
    prefix_here = prefix_lengths[group_ids]
    state_decode = decode_state
    state_prompt = fresh_state(prompt_count)
    req_count = lax.axis_size("req")
    context_rows = context_keys.shape[1]
    context_span = context_count * context_rows
    context_gathered = lax.all_gather(
        context_keys.reshape(context_span, heads_kv * HD), "req", axis=0, tiled=False
    )
    new_pack = jnp.concatenate(
        [context_values.reshape(context_span, heads_kv * HD), new_keys, new_values], 0
    )
    new_copies = jnp.broadcast_to(new_pack[None], (req_count,) + new_pack.shape)
    new_gathered = lax.all_to_all(
        new_copies.reshape(req_count * new_pack.shape[0], -1), "req", 0, 0, tiled=True
    ).reshape(req_count, new_pack.shape[0], -1)

    def context_of(source):
        piece = source[:, :context_span]
        piece = piece.reshape(req_count, context_count, context_rows, heads_kv * HD)
        return jnp.transpose(piece, (1, 0, 2, 3)).reshape(
            context_count, req_count * context_rows, heads_kv * HD
        )

    def prompt_of(offset):
        piece = new_gathered[:, offset : offset + rows_here][:, decode_count:]
        return piece.reshape(req_count * prompt_count, heads_kv * HD)

    key_block = context_of(context_gathered)
    value_block = context_of(new_gathered)
    extent = key_block.shape[1]
    positions = jnp.arange(extent)
    key_split = key_block.reshape(context_count, extent, heads_kv, HD)
    value_split = value_block.reshape(context_count, extent, heads_kv, HD)
    chosen_keys = key_split[group_ids]
    chosen_values = value_split[group_ids]
    block_scores = (
        jnp.einsum("ikgd,ickd->ikgc", query_decode, chosen_keys, preferred_element_type=jnp.float32)
        * scaling
    )
    block_usable = (positions[None, :] < prefix_here[:, None])[:, None, None, :]
    state_decode = absorb(
        state_decode, block_scores, block_usable, chosen_values, "ikgc,ickd->ikgd"
    )
    block_scores = (
        jnp.einsum(
            "jkgd,ckd->jkgc",
            query_prompt,
            key_split[context_count - 1],
            preferred_element_type=jnp.float32,
        )
        * scaling
    )
    block_usable = (positions < prompt_length)[None, None, None, :]
    state_prompt = absorb(
        state_prompt, block_scores, block_usable, value_split[context_count - 1], "jkgc,ckd->jkgd"
    )
    prompt_state = state_prompt
    own_positions = lax.axis_index("req") * prompt_count + jnp.arange(prompt_count, dtype=jnp.int32)
    key_block = prompt_of(context_span)
    value_block = prompt_of(context_span + rows_here)
    extent = key_block.shape[0]
    positions = jnp.arange(extent, dtype=jnp.int32)
    block_scores = (
        jnp.einsum(
            "jkgd,ckd->jkgc",
            query_prompt,
            key_block.reshape(extent, heads_kv, HD),
            preferred_element_type=jnp.float32,
        )
        * scaling
    )
    block_usable = (positions[None, :] <= own_positions[:, None])[:, None, None, :]
    prompt_state = absorb(
        prompt_state,
        block_scores,
        block_usable,
        value_block.reshape(extent, heads_kv, HD),
        "jkgc,ckd->jkgd",
    )

    def finish(carried):
        return (carried[2] / carried[1][..., None]).astype(jnp.bfloat16)

    attended = jnp.concatenate([finish(state_decode), finish(prompt_state)], 0).reshape(
        rows_here, heads_kv * group_size * HD
    )
    mlp_count = lax.axis_size("mlp")
    head_partial = jnp.dot(attended, out_weight, preferred_element_type=jnp.float32)
    pieces = lax.all_to_all(
        head_partial.astype(jnp.bfloat16), "mlp", 1, 0, tiled=True
    )
    projected = jnp.sum(
        pieces.reshape(mlp_count, rows_here, -1).astype(jnp.float32), axis=0
    )
    mixed = (resid.astype(jnp.float32) + projected).astype(jnp.bfloat16)
    mixed_wide = mixed.astype(jnp.float32)
    mixed_rows = lax.all_gather(mixed, "mlp", axis=1, tiled=True).astype(jnp.float32)
    square_total = jnp.sum(mixed_rows * mixed_rows, axis=1)
    half = D // 2
    side = lax.axis_index("mlp") % 2
    own_half = lax.dynamic_slice_in_dim(mixed_rows, side * half, half, axis=1)
    own_gain = lax.dynamic_slice_in_dim(norm_gain, side * half, half, axis=0)
    normed = (
        own_half * lax.rsqrt(square_total / D + 1e-06)[:, None] * own_gain[None, :]
    ).astype(jnp.bfloat16)
    near_rows = lax.all_gather(normed, "req", axis=0, tiled=True)
    pairs = [(i, i ^ 1) for i in range(mlp_count)]
    far_rows = lax.ppermute(near_rows, "mlp", pairs)

    def project(weight):
        near_weight = lax.dynamic_slice_in_dim(weight, side * half, half, axis=0)
        far_weight = lax.dynamic_slice_in_dim(weight, (1 - side) * half, half, axis=0)
        return jnp.dot(near_rows, near_weight, preferred_element_type=jnp.float32) + jnp.dot(
            far_rows, far_weight, preferred_element_type=jnp.float32
        )

    gate_proj = project(gate_weight)
    up_proj = project(up_weight)
    hidden = (jax.nn.silu(gate_proj) * up_proj).astype(jnp.bfloat16)
    hidden_block = lax.all_gather(hidden, "mlp", axis=1, tiled=True)
    down_partial = jnp.dot(hidden_block, down_weight, preferred_element_type=jnp.float32)
    req_pieces = lax.all_to_all(down_partial.astype(jnp.bfloat16), "req", 0, 0, tiled=True)
    feed = jnp.sum(
        req_pieces.reshape(req_count, rows_here, -1).astype(jnp.float32), axis=0
    )
    return (mixed_wide + feed).astype(jnp.bfloat16)


def solution(mesh):
    return jax.shard_map(
        per_device,
        mesh=mesh,
        in_specs=(
            P("req", "mlp"),
            P("req", "mlp"),
            P("req", "mlp"),
            P("req", "mlp"),
            P("req", None, "mlp"),
            P("req", None, "mlp"),
            P(None, "req", "mlp"),
            P(None, "req", "mlp"),
            P("req"),
            P("req"),
            P(),
            P(),
            P("mlp", None),
            P(),
            P(None, ("req", "mlp")),
            P(None, ("req", "mlp")),
            P("req", "mlp"),
        ),
        out_specs=P("req", "mlp"),
        check_vma=False,
    )
```

```python
import math

import jax
import jax.numpy as jnp
from jax import lax
from jax.sharding import PartitionSpec as P

D = 5120
HQ = 40
KV = 8
HD = 128


NEGATIVE = -1e30
REQ = ("ry", "rz")


def absorb(carried, scores, allowed, values, pattern):
    running, totals, summed = carried
    scores = jnp.where(allowed, scores, -jnp.inf)
    highest = jnp.maximum(running, jnp.max(scores, axis=-1))
    exponent = jnp.where(allowed, jnp.exp(scores - highest[..., None]), 0.0)
    fading = jnp.exp(running - highest)
    weights = exponent.astype(jnp.bfloat16)
    summed = summed * fading[..., None] + jnp.einsum(
        pattern, weights, values, preferred_element_type=jnp.float32
    )
    totals = totals * fading + jnp.sum(exponent, axis=-1)
    return (highest, totals, summed)


def per_device(
    resid,
    queries,
    new_keys,
    new_values,
    cache_keys,
    cache_values,
    context_keys,
    context_values,
    cache_lengths,
    group_ids,
    prefix_lengths,
    prompt_start,
    out_weight,
    norm_gain,
    gate_weight,
    up_weight,
    down_weight,
):
    rows_here = queries.shape[0]
    decode_count = cache_keys.shape[0]
    prompt_count = rows_here - decode_count
    heads_kv = new_keys.shape[1] // HD
    group_size = HQ // KV
    scaling = 1.0 / math.sqrt(HD)
    cache_span = cache_keys.shape[1]
    context_count = context_keys.shape[0]
    query_rows = queries.reshape(rows_here, heads_kv, group_size, HD)
    query_decode = query_rows[:decode_count]
    query_prompt = query_rows[decode_count:]
    key_rows = new_keys.reshape(rows_here, heads_kv, HD)
    value_rows = new_values.reshape(rows_here, heads_kv, HD)

    def fresh_state(row_count):
        return (
            jnp.full((row_count, heads_kv, group_size), NEGATIVE, jnp.float32),
            jnp.zeros((row_count, heads_kv, group_size), jnp.float32),
            jnp.zeros((row_count, heads_kv, group_size, HD), jnp.float32),
        )

    past_keys = cache_keys.reshape(decode_count, cache_span, heads_kv, HD)
    past_values = cache_values.reshape(decode_count, cache_span, heads_kv, HD)
    scores = (
        jnp.einsum("ikgd,ickd->ikgc", query_decode, past_keys, preferred_element_type=jnp.float32)
        * scaling
    )
    usable = (jnp.arange(cache_span)[None, :] < cache_lengths[:, None])[:, None, None, :]
    decode_state = absorb(fresh_state(decode_count), scores, usable, past_values, "ikgc,ickd->ikgd")
    own_scores = (
        jnp.einsum(
            "ikgd,ikd->ikg",
            query_decode,
            key_rows[:decode_count],
            preferred_element_type=jnp.float32,
        )[..., None]
        * scaling
    )
    decode_state = absorb(
        decode_state,
        own_scores,
        jnp.ones(own_scores.shape, dtype=bool),
        value_rows[:decode_count][:, None],
        "ikgc,ickd->ikgd",
    )
    prompt_length = prompt_start[0]
    prefix_here = prefix_lengths[group_ids]
    state_decode = decode_state
    state_prompt = fresh_state(prompt_count)
    req_count = lax.axis_size("ry") * lax.axis_size("rz")
    context_rows = context_keys.shape[1]
    context_pack = jnp.concatenate(
        [
            context_keys.reshape(context_count * context_rows, heads_kv * HD),
            context_values.reshape(context_count * context_rows, heads_kv * HD),
        ],
        0,
    )
    context_gathered = lax.all_gather(context_pack, REQ, axis=0, tiled=False)
    new_pack = jnp.concatenate([new_keys, new_values], 0)
    new_copies = jnp.broadcast_to(new_pack[None], (req_count,) + new_pack.shape)
    new_gathered = lax.all_to_all(
        new_copies.reshape(req_count * new_pack.shape[0], -1), REQ, 0, 0, tiled=True
    ).reshape(req_count, new_pack.shape[0], -1)
    context_span = context_count * context_rows

    def context_of(offset):
        piece = context_gathered[:, offset : offset + context_span]
        piece = piece.reshape(req_count, context_count, context_rows, heads_kv * HD)
        return jnp.transpose(piece, (1, 0, 2, 3)).reshape(
            context_count, req_count * context_rows, heads_kv * HD
        )

    def prompt_of(offset):
        piece = new_gathered[:, offset : offset + rows_here][:, decode_count:]
        return piece.reshape(req_count * prompt_count, heads_kv * HD)

    key_block = context_of(0)
    value_block = context_of(context_span)
    extent = key_block.shape[1]
    positions = jnp.arange(extent)
    key_split = key_block.reshape(context_count, extent, heads_kv, HD)
    value_split = value_block.reshape(context_count, extent, heads_kv, HD)
    chosen_keys = key_split[group_ids]
    chosen_values = value_split[group_ids]
    block_scores = (
        jnp.einsum("ikgd,ickd->ikgc", query_decode, chosen_keys, preferred_element_type=jnp.float32)
        * scaling
    )
    block_usable = (positions[None, :] < prefix_here[:, None])[:, None, None, :]
    state_decode = absorb(
        state_decode, block_scores, block_usable, chosen_values, "ikgc,ickd->ikgd"
    )
    block_scores = (
        jnp.einsum(
            "jkgd,ckd->jkgc",
            query_prompt,
            key_split[context_count - 1],
            preferred_element_type=jnp.float32,
        )
        * scaling
    )
    block_usable = (positions < prompt_length)[None, None, None, :]
    state_prompt = absorb(
        state_prompt, block_scores, block_usable, value_split[context_count - 1], "jkgc,ckd->jkgd"
    )
    prompt_state = state_prompt
    own_positions = (lax.axis_index("ry") * lax.axis_size("rz") + lax.axis_index("rz")) * prompt_count + jnp.arange(prompt_count, dtype=jnp.int32)
    key_block = prompt_of(0)
    value_block = prompt_of(rows_here)
    extent = key_block.shape[0]
    positions = jnp.arange(extent, dtype=jnp.int32)
    block_scores = (
        jnp.einsum(
            "jkgd,ckd->jkgc",
            query_prompt,
            key_block.reshape(extent, heads_kv, HD),
            preferred_element_type=jnp.float32,
        )
        * scaling
    )
    block_usable = (positions[None, :] <= own_positions[:, None])[:, None, None, :]
    prompt_state = absorb(
        prompt_state,
        block_scores,
        block_usable,
        value_block.reshape(extent, heads_kv, HD),
        "jkgc,ckd->jkgd",
    )

    def finish(carried):
        return (carried[2] / carried[1][..., None]).astype(jnp.bfloat16)

    attended = jnp.concatenate([finish(state_decode), finish(prompt_state)], 0).reshape(
        rows_here, heads_kv * group_size * HD
    )
    mlp_count = lax.axis_size("mlp")
    head_partial = jnp.dot(attended, out_weight, preferred_element_type=jnp.float32)
    pieces = lax.all_to_all(
        head_partial.astype(jnp.bfloat16), "mlp", 1, 0, tiled=True
    )
    projected = jnp.sum(
        pieces.reshape(mlp_count, rows_here, -1).astype(jnp.float32), axis=0
    )
    mixed = (resid.astype(jnp.float32) + projected).astype(jnp.bfloat16)
    mixed_wide = mixed.astype(jnp.float32)
    mixed_rows = lax.all_gather(mixed, "mlp", axis=1, tiled=True).astype(jnp.float32)
    square_total = jnp.sum(mixed_rows * mixed_rows, axis=1)
    half = D // 2
    side = lax.axis_index("mlp") % 2
    own_half = lax.dynamic_slice_in_dim(mixed_rows, side * half, half, axis=1)
    own_gain = lax.dynamic_slice_in_dim(norm_gain, side * half, half, axis=0)
    normed = (
        own_half * lax.rsqrt(square_total / D + 1e-06)[:, None] * own_gain[None, :]
    ).astype(jnp.bfloat16)
    near_rows = lax.all_gather(normed, REQ, axis=0, tiled=True)
    pairs = [(i, i ^ 1) for i in range(mlp_count)]
    far_rows = lax.ppermute(near_rows, "mlp", pairs)

    def project(weight):
        near_weight = lax.dynamic_slice_in_dim(weight, side * half, half, axis=0)
        far_weight = lax.dynamic_slice_in_dim(weight, (1 - side) * half, half, axis=0)
        return jnp.dot(near_rows, near_weight, preferred_element_type=jnp.float32) + jnp.dot(
            far_rows, far_weight, preferred_element_type=jnp.float32
        )

    gate_proj = project(gate_weight)
    up_proj = project(up_weight)
    hidden = (jax.nn.silu(gate_proj) * up_proj).astype(jnp.bfloat16)
    hidden_block = lax.all_gather(hidden, "mlp", axis=1, tiled=True)
    down_partial = jnp.dot(hidden_block, down_weight, preferred_element_type=jnp.float32)
    outer, inner = lax.axis_size("ry"), lax.axis_size("rz")
    by_owner = down_partial.astype(jnp.bfloat16).reshape(outer, inner, rows_here, -1)
    inner_pieces = lax.all_to_all(by_owner, "rz", 1, 1, tiled=True)
    inner_sum = jnp.sum(
        inner_pieces.reshape(outer, inner, rows_here, -1).astype(jnp.float32), axis=1
    ).astype(jnp.bfloat16)
    outer_pieces = lax.all_to_all(inner_sum, "ry", 0, 0, tiled=True)
    feed = jnp.sum(outer_pieces.astype(jnp.float32), axis=0)
    return (mixed_wide + feed).astype(jnp.bfloat16)


def solution(mesh):
    req_size, mlp_size = mesh.devices.shape
    split_mesh = jax.sharding.Mesh(
        mesh.devices.reshape(4, req_size // 4, mlp_size), ("ry", "rz", "mlp")
    )
    return jax.shard_map(
        per_device,
        mesh=split_mesh,
        in_specs=(
            P(REQ, "mlp"),
            P(REQ, "mlp"),
            P(REQ, "mlp"),
            P(REQ, "mlp"),
            P(REQ, None, "mlp"),
            P(REQ, None, "mlp"),
            P(None, REQ, "mlp"),
            P(None, REQ, "mlp"),
            P(REQ),
            P(REQ),
            P(),
            P(),
            P("mlp", None),
            P(),
            P(None, ("ry", "rz", "mlp")),
            P(None, ("ry", "rz", "mlp")),
            P(REQ, "mlp"),
        ),
        out_specs=P(REQ, "mlp"),
        check_vma=False,
    )
```

```python
import math

import jax
import jax.numpy as jnp
from jax import lax
from jax.sharding import PartitionSpec as P

D = 5120
HQ = 40
KV = 8
HD = 128


NEGATIVE = -1e30


def absorb(carried, scores, allowed, values, pattern):
    running, totals, summed = carried
    scores = jnp.where(allowed, scores, -jnp.inf)
    highest = jnp.maximum(running, jnp.max(scores, axis=-1))
    exponent = jnp.where(allowed, jnp.exp(scores - highest[..., None]), 0.0)
    fading = jnp.exp(running - highest)
    weights = exponent.astype(jnp.bfloat16)
    summed = summed * fading[..., None] + jnp.einsum(
        pattern, weights, values, preferred_element_type=jnp.float32
    )
    totals = totals * fading + jnp.sum(exponent, axis=-1)
    return (highest, totals, summed)


def per_device(
    resid,
    queries,
    new_keys,
    new_values,
    cache_keys,
    cache_values,
    context_keys,
    context_values,
    cache_lengths,
    group_ids,
    prefix_lengths,
    prompt_start,
    out_weight,
    norm_gain,
    gate_weight,
    up_weight,
    down_weight,
):
    rows_here = queries.shape[0]
    decode_count = cache_keys.shape[0]
    prompt_count = rows_here - decode_count
    heads_kv = new_keys.shape[1] // HD
    group_size = HQ // KV
    scaling = 1.0 / math.sqrt(HD)
    cache_span = cache_keys.shape[1]
    context_count = context_keys.shape[0]
    query_rows = queries.reshape(rows_here, heads_kv, group_size, HD)
    query_decode = query_rows[:decode_count]
    query_prompt = query_rows[decode_count:]
    key_rows = new_keys.reshape(rows_here, heads_kv, HD)
    value_rows = new_values.reshape(rows_here, heads_kv, HD)

    def fresh_state(row_count):
        return (
            jnp.full((row_count, heads_kv, group_size), NEGATIVE, jnp.float32),
            jnp.zeros((row_count, heads_kv, group_size), jnp.float32),
            jnp.zeros((row_count, heads_kv, group_size, HD), jnp.float32),
        )

    past_keys = cache_keys.reshape(decode_count, cache_span, heads_kv, HD)
    past_values = cache_values.reshape(decode_count, cache_span, heads_kv, HD)
    scores = (
        jnp.einsum("ikgd,ickd->ikgc", query_decode, past_keys, preferred_element_type=jnp.float32)
        * scaling
    )
    usable = (jnp.arange(cache_span)[None, :] < cache_lengths[:, None])[:, None, None, :]
    decode_state = absorb(fresh_state(decode_count), scores, usable, past_values, "ikgc,ickd->ikgd")
    own_scores = (
        jnp.einsum(
            "ikgd,ikd->ikg",
            query_decode,
            key_rows[:decode_count],
            preferred_element_type=jnp.float32,
        )[..., None]
        * scaling
    )
    decode_state = absorb(
        decode_state,
        own_scores,
        jnp.ones(own_scores.shape, dtype=bool),
        value_rows[:decode_count][:, None],
        "ikgc,ickd->ikgd",
    )
    prompt_length = prompt_start[0]
    prefix_here = prefix_lengths[group_ids]
    state_decode = decode_state
    state_prompt = fresh_state(prompt_count)
    req_count = lax.axis_size("req")
    context_rows = context_keys.shape[1]
    context_pack = jnp.concatenate(
        [
            context_keys.reshape(context_count * context_rows, heads_kv * HD),
            context_values.reshape(context_count * context_rows, heads_kv * HD),
        ],
        0,
    )
    context_gathered = lax.all_gather(context_pack, "req", axis=0, tiled=False)
    new_pack = jnp.concatenate([new_keys, new_values], 0)
    new_copies = jnp.broadcast_to(new_pack[None], (req_count,) + new_pack.shape)
    new_gathered = lax.all_to_all(
        new_copies.reshape(req_count * new_pack.shape[0], -1), "req", 0, 0, tiled=True
    ).reshape(req_count, new_pack.shape[0], -1)
    context_span = context_count * context_rows

    def context_of(offset):
        piece = context_gathered[:, offset : offset + context_span]
        piece = piece.reshape(req_count, context_count, context_rows, heads_kv * HD)
        return jnp.transpose(piece, (1, 0, 2, 3)).reshape(
            context_count, req_count * context_rows, heads_kv * HD
        )

    def prompt_of(offset):
        piece = new_gathered[:, offset : offset + rows_here][:, decode_count:]
        return piece.reshape(req_count * prompt_count, heads_kv * HD)

    key_block = context_of(0)
    value_block = context_of(context_span)
    extent = key_block.shape[1]
    positions = jnp.arange(extent)
    key_split = key_block.reshape(context_count, extent, heads_kv, HD)
    value_split = value_block.reshape(context_count, extent, heads_kv, HD)
    chosen_keys = key_split[group_ids]
    chosen_values = value_split[group_ids]
    block_scores = (
        jnp.einsum("ikgd,ickd->ikgc", query_decode, chosen_keys, preferred_element_type=jnp.float32)
        * scaling
    )
    block_usable = (positions[None, :] < prefix_here[:, None])[:, None, None, :]
    state_decode = absorb(
        state_decode, block_scores, block_usable, chosen_values, "ikgc,ickd->ikgd"
    )
    block_scores = (
        jnp.einsum(
            "jkgd,ckd->jkgc",
            query_prompt,
            key_split[context_count - 1],
            preferred_element_type=jnp.float32,
        )
        * scaling
    )
    block_usable = (positions < prompt_length)[None, None, None, :]
    state_prompt = absorb(
        state_prompt, block_scores, block_usable, value_split[context_count - 1], "jkgc,ckd->jkgd"
    )
    prompt_state = state_prompt
    own_positions = lax.axis_index("req") * prompt_count + jnp.arange(prompt_count, dtype=jnp.int32)
    key_block = prompt_of(0)
    value_block = prompt_of(rows_here)
    extent = key_block.shape[0]
    positions = jnp.arange(extent, dtype=jnp.int32)
    block_scores = (
        jnp.einsum(
            "jkgd,ckd->jkgc",
            query_prompt,
            key_block.reshape(extent, heads_kv, HD),
            preferred_element_type=jnp.float32,
        )
        * scaling
    )
    block_usable = (positions[None, :] <= own_positions[:, None])[:, None, None, :]
    prompt_state = absorb(
        prompt_state,
        block_scores,
        block_usable,
        value_block.reshape(extent, heads_kv, HD),
        "jkgc,ckd->jkgd",
    )

    def finish(carried):
        return (carried[2] / carried[1][..., None]).astype(jnp.bfloat16)

    attended = jnp.concatenate([finish(state_decode), finish(prompt_state)], 0).reshape(
        rows_here, heads_kv * group_size * HD
    )
    mlp_count = lax.axis_size("mlp")
    head_partial = jnp.dot(attended, out_weight, preferred_element_type=jnp.float32)
    pieces = lax.all_to_all(
        head_partial.astype(jnp.bfloat16), "mlp", 1, 0, tiled=True
    )
    projected = jnp.sum(
        pieces.reshape(mlp_count, rows_here, -1).astype(jnp.float32), axis=0
    )
    mixed = (resid.astype(jnp.float32) + projected).astype(jnp.bfloat16)
    mixed_wide = mixed.astype(jnp.float32)
    mixed_rows = lax.all_gather(mixed, "mlp", axis=1, tiled=True).astype(jnp.float32)
    square_total = jnp.sum(mixed_rows * mixed_rows, axis=1)
    half = D // 2
    side = lax.axis_index("mlp") % 2
    own_half = lax.dynamic_slice_in_dim(mixed_rows, side * half, half, axis=1)
    own_gain = lax.dynamic_slice_in_dim(norm_gain, side * half, half, axis=0)
    normed = (
        own_half * lax.rsqrt(square_total / D + 1e-06)[:, None] * own_gain[None, :]
    ).astype(jnp.bfloat16)
    near_rows = lax.all_gather(normed, "req", axis=0, tiled=True)
    pairs = [(i, i ^ 1) for i in range(mlp_count)]
    far_rows = lax.ppermute(near_rows, "mlp", pairs)

    def project(weight):
        near_weight = lax.dynamic_slice_in_dim(weight, side * half, half, axis=0)
        far_weight = lax.dynamic_slice_in_dim(weight, (1 - side) * half, half, axis=0)
        return jnp.dot(near_rows, near_weight, preferred_element_type=jnp.float32) + jnp.dot(
            far_rows, far_weight, preferred_element_type=jnp.float32
        )

    width = gate_weight.shape[1]
    both_proj = project(jnp.concatenate([gate_weight, up_weight], 1))
    gate_proj = both_proj[:, :width]
    up_proj = both_proj[:, width:]
    hidden = (jax.nn.silu(gate_proj) * up_proj).astype(jnp.bfloat16)
    hidden_block = lax.all_gather(hidden, "mlp", axis=1, tiled=True)
    down_partial = jnp.dot(hidden_block, down_weight, preferred_element_type=jnp.float32)
    req_pieces = lax.all_to_all(down_partial.astype(jnp.bfloat16), "req", 0, 0, tiled=True)
    feed = jnp.sum(
        req_pieces.reshape(req_count, rows_here, -1).astype(jnp.float32), axis=0
    )
    return (mixed_wide + feed).astype(jnp.bfloat16)


def solution(mesh):
    return jax.shard_map(
        per_device,
        mesh=mesh,
        in_specs=(
            P("req", "mlp"),
            P("req", "mlp"),
            P("req", "mlp"),
            P("req", "mlp"),
            P("req", None, "mlp"),
            P("req", None, "mlp"),
            P(None, "req", "mlp"),
            P(None, "req", "mlp"),
            P("req"),
            P("req"),
            P(),
            P(),
            P("mlp", None),
            P(),
            P(None, ("req", "mlp")),
            P(None, ("req", "mlp")),
            P("req", "mlp"),
        ),
        out_specs=P("req", "mlp"),
        check_vma=False,
    )
```

```python
import math

import jax
import jax.numpy as jnp
from jax import lax
from jax.sharding import PartitionSpec as P

D = 5120
HQ = 40
KV = 8
HD = 128


NEGATIVE = -1e30


def absorb(carried, scores, allowed, values, pattern):
    running, totals, summed = carried
    scores = jnp.where(allowed, scores, -jnp.inf)
    highest = jnp.maximum(running, jnp.max(scores, axis=-1))
    exponent = jnp.where(allowed, jnp.exp(scores - highest[..., None]), 0.0)
    fading = jnp.exp(running - highest)
    weights = exponent.astype(jnp.bfloat16)
    summed = summed * fading[..., None] + jnp.einsum(
        pattern, weights, values, preferred_element_type=jnp.float32
    )
    totals = totals * fading + jnp.sum(exponent, axis=-1)
    return (highest, totals, summed)


def per_device(
    resid,
    queries,
    new_keys,
    new_values,
    cache_keys,
    cache_values,
    context_keys,
    context_values,
    cache_lengths,
    group_ids,
    prefix_lengths,
    prompt_start,
    out_weight,
    norm_gain,
    gate_weight,
    up_weight,
    down_weight,
):
    rows_here = queries.shape[0]
    decode_count = cache_keys.shape[0]
    prompt_count = rows_here - decode_count
    heads_kv = new_keys.shape[1] // HD
    group_size = HQ // KV
    scaling = 1.0 / math.sqrt(HD)
    cache_span = cache_keys.shape[1]
    context_count = context_keys.shape[0]
    query_rows = queries.reshape(rows_here, heads_kv, group_size, HD)
    query_decode = query_rows[:decode_count]
    query_prompt = query_rows[decode_count:]
    key_rows = new_keys.reshape(rows_here, heads_kv, HD)
    value_rows = new_values.reshape(rows_here, heads_kv, HD)

    def fresh_state(row_count):
        return (
            jnp.full((row_count, heads_kv, group_size), NEGATIVE, jnp.float32),
            jnp.zeros((row_count, heads_kv, group_size), jnp.float32),
            jnp.zeros((row_count, heads_kv, group_size, HD), jnp.float32),
        )

    past_keys = cache_keys.reshape(decode_count, cache_span, heads_kv, HD)
    past_values = cache_values.reshape(decode_count, cache_span, heads_kv, HD)
    scores = (
        jnp.einsum("ikgd,ickd->ikgc", query_decode, past_keys, preferred_element_type=jnp.float32)
        * scaling
    )
    usable = (jnp.arange(cache_span)[None, :] < cache_lengths[:, None])[:, None, None, :]
    decode_state = absorb(fresh_state(decode_count), scores, usable, past_values, "ikgc,ickd->ikgd")
    own_scores = (
        jnp.einsum(
            "ikgd,ikd->ikg",
            query_decode,
            key_rows[:decode_count],
            preferred_element_type=jnp.float32,
        )[..., None]
        * scaling
    )
    decode_state = absorb(
        decode_state,
        own_scores,
        jnp.ones(own_scores.shape, dtype=bool),
        value_rows[:decode_count][:, None],
        "ikgc,ickd->ikgd",
    )
    prompt_length = prompt_start[0]
    prefix_here = prefix_lengths[group_ids]
    state_decode = decode_state
    state_prompt = fresh_state(prompt_count)
    req_count = lax.axis_size("req")
    context_rows = context_keys.shape[1]
    context_pack = jnp.concatenate(
        [
            context_keys.reshape(context_count * context_rows, heads_kv * HD),
            context_values.reshape(context_count * context_rows, heads_kv * HD),
        ],
        0,
    )
    context_gathered = lax.all_gather(context_pack, "req", axis=0, tiled=False)
    new_pack = jnp.concatenate([new_keys, new_values], 0)
    new_copies = jnp.broadcast_to(new_pack[None], (req_count,) + new_pack.shape)
    new_gathered = lax.all_to_all(
        new_copies.reshape(req_count * new_pack.shape[0], -1), "req", 0, 0, tiled=True
    ).reshape(req_count, new_pack.shape[0], -1)
    context_span = context_count * context_rows

    def context_of(offset):
        piece = context_gathered[:, offset : offset + context_span]
        piece = piece.reshape(req_count, context_count, context_rows, heads_kv * HD)
        return jnp.transpose(piece, (1, 0, 2, 3)).reshape(
            context_count, req_count * context_rows, heads_kv * HD
        )

    def prompt_of(offset):
        piece = new_gathered[:, offset : offset + rows_here][:, decode_count:]
        return piece.reshape(req_count * prompt_count, heads_kv * HD)

    key_block = context_of(0)
    value_block = context_of(context_span)
    extent = key_block.shape[1]
    positions = jnp.arange(extent)
    key_split = key_block.reshape(context_count, extent, heads_kv, HD)
    value_split = value_block.reshape(context_count, extent, heads_kv, HD)
    chosen_keys = key_split[group_ids]
    chosen_values = value_split[group_ids]
    block_scores = (
        jnp.einsum("ikgd,ickd->ikgc", query_decode, chosen_keys, preferred_element_type=jnp.float32)
        * scaling
    )
    block_usable = (positions[None, :] < prefix_here[:, None])[:, None, None, :]
    state_decode = absorb(
        state_decode, block_scores, block_usable, chosen_values, "ikgc,ickd->ikgd"
    )
    block_scores = (
        jnp.einsum(
            "jkgd,ckd->jkgc",
            query_prompt,
            key_split[context_count - 1],
            preferred_element_type=jnp.float32,
        )
        * scaling
    )
    block_usable = (positions < prompt_length)[None, None, None, :]
    state_prompt = absorb(
        state_prompt, block_scores, block_usable, value_split[context_count - 1], "jkgc,ckd->jkgd"
    )
    prompt_state = state_prompt
    own_positions = lax.axis_index("req") * prompt_count + jnp.arange(prompt_count, dtype=jnp.int32)
    key_block = prompt_of(0)
    value_block = prompt_of(rows_here)
    extent = key_block.shape[0]
    positions = jnp.arange(extent, dtype=jnp.int32)
    block_scores = (
        jnp.einsum(
            "jkgd,ckd->jkgc",
            query_prompt,
            key_block.reshape(extent, heads_kv, HD),
            preferred_element_type=jnp.float32,
        )
        * scaling
    )
    block_usable = (positions[None, :] <= own_positions[:, None])[:, None, None, :]
    prompt_state = absorb(
        prompt_state,
        block_scores,
        block_usable,
        value_block.reshape(extent, heads_kv, HD),
        "jkgc,ckd->jkgd",
    )

    def finish(carried):
        return (carried[2] / carried[1][..., None]).astype(jnp.bfloat16)

    attended = jnp.concatenate([finish(state_decode), finish(prompt_state)], 0).reshape(
        rows_here, heads_kv * group_size * HD
    )
    mlp_count = lax.axis_size("mlp")
    head_partial = jnp.dot(attended, out_weight, preferred_element_type=jnp.float32)
    pieces = lax.all_to_all(
        head_partial.astype(jnp.bfloat16), "mlp", 1, 0, tiled=True
    )
    projected = jnp.sum(
        pieces.reshape(mlp_count, rows_here, -1).astype(jnp.float32), axis=0
    )
    mixed = (resid.astype(jnp.float32) + projected).astype(jnp.bfloat16)
    mixed_wide = mixed.astype(jnp.float32)
    mixed_rows = lax.all_gather(mixed, "mlp", axis=1, tiled=True).astype(jnp.float32)
    square_total = jnp.sum(mixed_rows * mixed_rows, axis=1)
    half = D // 2
    side = lax.axis_index("mlp") % 2
    own_half = lax.dynamic_slice_in_dim(mixed_rows, side * half, half, axis=1)
    own_gain = lax.dynamic_slice_in_dim(norm_gain, side * half, half, axis=0)
    normed = (
        own_half * lax.rsqrt(square_total / D + 1e-06)[:, None] * own_gain[None, :]
    ).astype(jnp.bfloat16)
    near_rows = lax.all_gather(normed, "req", axis=0, tiled=True)
    pairs = [(i, i ^ 1) for i in range(mlp_count)]
    quarter = half // 2
    far_parts = [
        lax.ppermute(near_rows[:, :quarter], "mlp", pairs),
        lax.ppermute(near_rows[:, quarter:], "mlp", pairs),
    ]

    def project(weight):
        near_weight = lax.dynamic_slice_in_dim(weight, side * half, half, axis=0)
        far_weight = lax.dynamic_slice_in_dim(weight, (1 - side) * half, half, axis=0)
        total = jnp.dot(near_rows, near_weight, preferred_element_type=jnp.float32)
        total = total + jnp.dot(
            far_parts[0], far_weight[:quarter], preferred_element_type=jnp.float32
        )
        return total + jnp.dot(
            far_parts[1], far_weight[quarter:], preferred_element_type=jnp.float32
        )

    width = gate_weight.shape[1]
    both_proj = project(jnp.concatenate([gate_weight, up_weight], 1))
    gate_proj = both_proj[:, :width]
    up_proj = both_proj[:, width:]
    hidden = (jax.nn.silu(gate_proj) * up_proj).astype(jnp.bfloat16)
    hidden_block = lax.all_gather(hidden, "mlp", axis=1, tiled=True)
    down_partial = jnp.dot(hidden_block, down_weight, preferred_element_type=jnp.float32)
    req_pieces = lax.all_to_all(down_partial.astype(jnp.bfloat16), "req", 0, 0, tiled=True)
    feed = jnp.sum(
        req_pieces.reshape(req_count, rows_here, -1).astype(jnp.float32), axis=0
    )
    return (mixed_wide + feed).astype(jnp.bfloat16)


def solution(mesh):
    return jax.shard_map(
        per_device,
        mesh=mesh,
        in_specs=(
            P("req", "mlp"),
            P("req", "mlp"),
            P("req", "mlp"),
            P("req", "mlp"),
            P("req", None, "mlp"),
            P("req", None, "mlp"),
            P(None, "req", "mlp"),
            P(None, "req", "mlp"),
            P("req"),
            P("req"),
            P(),
            P(),
            P("mlp", None),
            P(),
            P(None, ("req", "mlp")),
            P(None, ("req", "mlp")),
            P("req", "mlp"),
        ),
        out_specs=P("req", "mlp"),
        check_vma=False,
    )
```
